256 devices in a mesh: req: 8 (over z), head: 8 (over y, core), blk: 4 (over x).
Axes of the slice: x: 4, y: 4, z: 8, core: 2. Of those that a mesh axis runs over, the one named last changes fastest.
Arguments:
- queries: bfloat16 [4096, 4096], P(('req', 'blk'), 'head'), may hold values from -360 to 360
- span_kv: bfloat16 [4096, 8, 128], P(('req', 'blk'), 'head'), may hold values from -5 to 5
- cache_kv: bfloat16 [8, 8, 8192, 128], P('req', 'head', 'blk'), may hold values from -5 to 5
- prefix_len: int32 [8], P('req'), may hold values from 0 to 8192, as said below
- span_len: int32 [8], P('req'), may hold values from 1 to 512, as said below
- sinks: float32 [64], P('head'), may hold values from 0 to 4
- out_proj: bfloat16 [4096, 2880], P('head'), may hold values from -2 to 2
- residual: bfloat16 [4096, 2880], P(('req', 'blk')), may hold values from -3 to 3
- norm_gain: float32 [2880], replicated, may hold values from 0.1 to 1.9
- expert_ids: int32 [4096, 4], P(('req', 'blk')), may hold values from 0 to 31, all different within a row; in each aligned block of 128 rows (0 to 127, 128 to 255, ...) at most 32 rows name the same one
- expert_weights: float32 [4096, 4], P(('req', 'blk')), may hold values from 0.1 to 0.6
- w_gate: bfloat16 [32, 2880, 2880], P(('req', 'blk'), None, 'head'), may hold values from -0.3125 to 0.3125
- w_up: bfloat16 [32, 2880, 2880], P(('req', 'blk'), None, 'head'), may hold values from -0.3125 to 0.3125
- w_down: bfloat16 [32, 2880, 2880], P(('req', 'blk'), 'head'), may hold values from -0.02734375 to 0.02734375
- finished_pages: bfloat16 [1024, 1, 8, 128, 128], P(('req', 'blk'), None, 'head'), may hold values from -5 to 5
- page_table: int32 [1024], replicated, may hold values from 0 to 1023, as said below
Outputs:
- layer_out: bfloat16 [4096, 2880], P(('req', 'blk'), 'head')
- moved_pages: bfloat16 [1024, 1, 8, 128, 128], P(('req', 'blk'), None, 'head')
The draws below stay inside these ranges and needn't reach their ends.
Inputs may be any that keep to these rules, and one draw needn't show every extreme that they name: `prefix_len`: some request has exactly 8192 cached positions in use. `span_len`: some request has exactly 512 new tokens. `expert_ids`: each token names 4 different experts; within the 128 rows of one device no expert is named more than 32 times, and on some device one expert is named exactly 32 times. `page_table`: a permutation; for source block s (pages s*32 to (s+1)*32 - 1) and destination block d (rows d*32 to (d+1)*32 - 1), exactly 1 pages of s go to rows of d.
All inputs are finite; a program needn't handle non-finite values.
Results may differ from the reference program's by a relative error of at most 0.02.
Values may be sent and summed in bfloat16 or wider, within the bound.
No kernel may reach another device: no remote copies, remote signals or barrier semaphores. Data moves between devices by JAX's collectives and lax.ppermute only.
A program may use at most 192 MiB of HBM per device.

```python
import math
import jax
import jax.numpy as jnp
import numpy as np
from jax import lax

D = 2880
FF = 2880
HD = 64
QH = 64
KVH = 8
TOP = 4
SPAN = 512
PMAX = 8192
PAGE = 128
LAYERS = 1
PER_PAIR = 1
GROUP = 8
REQS = 8
TOKENS = 4096
TOK_DEV = 128
EXPERTS = 32
CAP = 32
FF_PART = 360
NPAGES = 1024
N_REQ = 8
N_HEAD = 8
N_BLK = 4


WINDOW_CAP = 64


def prefix_values(key):
    key_values, key_longest = jax.random.split(jax.random.fold_in(key, 41))
    values = jax.random.randint(key_values, (REQS,), 0, PMAX + 1)
    longest = jax.random.randint(key_longest, (), 0, REQS)
    return jnp.where(jnp.arange(REQS) == longest, PMAX, values).astype(jnp.int32)


def early_cache(key):
    window = min(WINDOW_CAP, PMAX)
    key_early = jax.random.fold_in(jax.random.fold_in(key, 61), 0)
    early = jnp.clip(jax.random.normal(key_early, (REQS, KVH, window, 2 * HD), jnp.float32), -5.0, 5.0)
    key_part = early[..., :HD]
    value_part = early[..., HD:]
    return (key_part, value_part)


def draw_queries(key, part):
    key_queries = jax.random.fold_in(key, 31)
    group_size = QH // KVH
    query_rows = jnp.clip(jax.random.normal(key_queries, (TOKENS, KVH, group_size, HD), jnp.float32), -5.0, 5.0)
    return query_rows.reshape(TOKENS, QH * HD).astype(jnp.bfloat16)


def draw_span_kv(key, part):
    key_keys, key_values = jax.random.split(jax.random.fold_in(key, 33))
    key_rows = jnp.clip(jax.random.normal(key_keys, (TOKENS, KVH, HD), jnp.float32), -5.0, 5.0)
    value_rows = jnp.clip(jax.random.normal(key_values, (TOKENS, KVH, HD), jnp.float32), -5.0, 5.0)
    return jnp.concatenate([key_rows, value_rows], -1).astype(jnp.bfloat16)


def draw_cache_kv(key, part):
    window = min(WINDOW_CAP, PMAX)
    key_part, value_part = early_cache(key)
    later = jnp.clip(jax.random.normal(jax.random.fold_in(key, 62), (REQS, KVH, PMAX - window, 2 * HD), jnp.float32), -5.0, 5.0)
    early = jnp.concatenate([key_part, value_part], -1)
    return jnp.concatenate([early, later], 2).astype(jnp.bfloat16)


def draw_prefix_len(key, part):
    return prefix_values(key)


def draw_span_len(key, part):
    key_values, key_longest = jax.random.split(jax.random.fold_in(key, 43))
    values = jax.random.randint(key_values, (REQS,), 1, SPAN + 1)
    longest = jax.random.randint(key_longest, (), 0, REQS)
    return jnp.where(jnp.arange(REQS) == longest, SPAN, values).astype(jnp.int32)


def draw_page_table(key, part):
    src_count = N_REQ * N_BLK
    pages_dev = PER_PAIR * src_count
    targets = jnp.arange(pages_dev, dtype=jnp.int32) // PER_PAIR
    dest_keys = jax.random.split(jax.random.fold_in(key, 51), src_count)
    destination = jax.vmap(lambda one_key: jax.random.permutation(one_key, targets))(dest_keys)
    onehot = (destination[:, :, None] == jnp.arange(src_count, dtype=jnp.int32)[None, None, :]).astype(jnp.int32)
    occurrence = jnp.sum((jnp.cumsum(onehot, 1) - onehot) * onehot, 2)
    arrival = jnp.arange(src_count, dtype=jnp.int32)[:, None] * PER_PAIR + occurrence
    slot_keys = jax.random.split(jax.random.fold_in(key, 52), src_count)
    shuffles = jax.vmap(lambda one_key: jax.random.permutation(one_key, jnp.arange(pages_dev, dtype=jnp.int32)))(slot_keys)
    slots = destination * pages_dev + shuffles[destination, arrival]
    return slots.reshape(-1).astype(jnp.int32)


def block_scale(own_key, dims, cuts, smallest, top_value):
    factor_of, own = 1.0, jax.random.fold_in(own_key, 6)
    for axis_at, shards_of in cuts:
        steps = jnp.exp(jax.random.uniform(jax.random.fold_in(own, axis_at), (shards_of,), jnp.float32, smallest / len(cuts), top_value / len(cuts)))
        factor_of = factor_of * jnp.repeat(steps, dims[axis_at] // shards_of).reshape([-1 if axis == axis_at else 1 for axis in range(len(dims))])
    return factor_of


def routed_block(rng, own, number, rows, amount, top, most, slope):
    order = jax.random.permutation(rng, amount)
    packed, ordinary = shares(amount, rows * top, most, slope, True), shares(amount, rows * top, most, slope, False)
    places = jnp.arange(amount)

    def named(tallies, rotation):
        used = int((tallies > 0).sum())
        fixed = max(1, used // 4)
        shifted = fixed + (places - fixed + rotation * (used - fixed)) % max(1, amount - fixed)
        return jnp.zeros((amount,), jnp.int32).at[order[jnp.where(places < fixed, places, shifted)]].set(jnp.asarray(tallies, jnp.int32))

    tallies = jnp.where(number % 4 == 0, named(packed, number // 4), named(ordinary, number - number // 4 - 1))
    mixed = jax.random.permutation(jax.random.fold_in(own, 3), amount)
    giver, taker = mixed[0:amount // 2 * 2:2], mixed[1:amount // 2 * 2:2]
    margin = jnp.minimum(tallies[giver] - 1, most - tallies[taker]) // 2
    margin = jnp.where((giver == order[0]) | (taker == order[0]) | (tallies[taker] == 0), 0, jnp.maximum(margin, 0))
    shifted = jax.random.randint(jax.random.fold_in(own, 4), (amount // 2,), 0, 1 << 20) % (margin + 1)
    tallies = tallies.at[giver].add(-shifted).at[taker].add(shifted)
    labels = jnp.searchsorted(jnp.cumsum(tallies), jnp.arange(rows * top), side="right").astype(jnp.int32)
    grid = labels.reshape(top, rows).T
    grid = grid[jax.random.permutation(jax.random.fold_in(own, 1), rows)]
    rotation = jax.random.randint(jax.random.fold_in(own, 2), (rows, 1), 0, top)
    return jnp.take_along_axis(grid, (jnp.arange(top)[None, :] + rotation) % top, axis=1)


def shares(amount, total, bound, slope, full):
    weights = [(1 << 20) // math.isqrt(rank ** slope) + 1 for rank in range(1, amount + 1)]
    largest = bound if full else min(bound, max(-(-total // amount), total * weights[0] // sum(weights)))
    least = 1 if total - largest >= amount - 1 else 0
    given, surplus = [largest] + [least] * (amount - 1), total - largest - least * (amount - 1)
    while surplus > 0:
        free = [i for i in range(1, amount) if given[i] < largest] or [i for i in range(1, amount) if given[i] < bound]
        pool, budget = sum([weights[i] for i in free]), surplus
        for i in free:
            extra = min(bound - given[i], max(1, budget * weights[i] // pool), surplus)
            given[i] = given[i] + extra
            surplus = surplus - extra
    return np.array(given)


def centred(stream_key, shape, spread, limit, shards=(), held_as=jnp.bfloat16):
    values = jax.random.normal(stream_key, shape, jnp.float32) * spread
    if len(shards) > 0:
        values = block_scale(stream_key, shape, shards, -0.22, 0.18) * values
    return jnp.clip(values, min=-limit, max=limit).astype(held_as)


def setup_inputs(seed: int = 0) -> dict:
    seeds = jax.random.split(jax.random.key(seed), 17)
    queries = draw_queries(jax.random.fold_in(seeds[16], 71), 0)
    span_kv = draw_span_kv(jax.random.fold_in(seeds[16], 71), 0)
    cache_kv = draw_cache_kv(jax.random.fold_in(seeds[16], 71), 0)
    prefix_len = draw_prefix_len(jax.random.fold_in(seeds[16], 71), 0)
    span_len = draw_span_len(jax.random.fold_in(seeds[16], 71), 0)
    sinks = jnp.clip(4.0 * jax.random.uniform(seeds[5], (QH,), jnp.float32) ** block_scale(seeds[5], (QH,), ((0, 8),), -0.2, 0.2), 0.0, 4.0)
    out_proj = centred(seeds[6], (QH * HD, D), (max(1, QH * HD // 512)) ** -0.5, 2.0, ((0, 8),))
    residual = centred(seeds[7], (TOKENS, D), 0.5, 3.0, ((0, 32),))
    norm_gain = jnp.clip(1.0 + 0.18 * jax.random.normal(seeds[8], (D,), jnp.float32), 0.1, 1.9)
    expert_ids_keys = jax.random.split(jax.random.fold_in(seeds[9], 1), TOKENS // TOK_DEV)
    expert_ids_turns = jax.random.permutation(jax.random.fold_in(seeds[9], 3), TOKENS // TOK_DEV)
    expert_ids = jax.vmap(lambda own, number: routed_block(jax.random.fold_in(seeds[9], 2), own, number, TOK_DEV, EXPERTS, TOP, CAP, 2))(expert_ids_keys, expert_ids_turns).reshape((TOKENS, TOP))
    expert_weights = jnp.clip(0.1 + 0.5 * jax.random.uniform(seeds[10], (TOKENS, TOP), jnp.float32) ** block_scale(seeds[10], (TOKENS, TOP), ((0, 32),), -0.2, 0.2), 0.1, 0.6)
    w_gate = centred(seeds[11], (EXPERTS, D, FF), (D // 9) ** -0.5, 0.3125, ((0, 32), (2, 8)))
    w_up = centred(seeds[12], (EXPERTS, D, FF), (D // 9) ** -0.5, 0.3125, ((0, 32), (2, 8)))
    w_down = centred(seeds[13], (EXPERTS, FF, D), (FF * 16) ** -0.5, 0.02734375, ((0, 32), (1, 8)))
    finished_pages = centred(seeds[14], (NPAGES, LAYERS, KVH, PAGE, 2 * HD), 1.0, 5.0, ((0, 32), (2, 8)))
    page_table = draw_page_table(jax.random.fold_in(seeds[16], 71), 0)
    return {"queries": queries, "span_kv": span_kv, "cache_kv": cache_kv, "prefix_len": prefix_len, "span_len": span_len, "sinks": sinks, "out_proj": out_proj, "residual": residual, "norm_gain": norm_gain, "expert_ids": expert_ids, "expert_weights": expert_weights, "w_gate": w_gate, "w_up": w_up, "w_down": w_down, "finished_pages": finished_pages, "page_table": page_table}


NEG_FILL = -1e+30

def attend_request(query_block, key_rows, sink_logit, prefix_count, span_count):
    head_dim = query_block.shape[-1]
    score_scale = head_dim ** (-0.5)
    key_total = key_rows.shape[1]
    block_len = math.gcd(128, math.gcd(PMAX, SPAN))
    block_count = key_total // block_len
    blocks = jnp.moveaxis(key_rows.reshape(KVH, block_count, block_len, 2 * head_dim), 1, 0)
    positions = jnp.arange(SPAN, dtype=jnp.int32)
    query_wide = query_block.astype(jnp.float32)

    def scores_of(key_block, block_index):
        scores = jnp.einsum('qhgd,hkd->qhgk', query_wide, key_block[..., :head_dim].astype(jnp.float32)) * score_scale
        key_pos = block_index * block_len + jnp.arange(block_len, dtype=jnp.int32)
        in_cache = jnp.broadcast_to((key_pos < prefix_count)[None, :], (SPAN, block_len))
        in_span = key_pos[None, :] - PMAX <= positions[:, None]
        allowed = jnp.where((key_pos < PMAX)[None, :], in_cache, in_span)
        return (scores, allowed[:, None, None, :])

    def first_pass(running_max, scan_item):
        scores, allowed = scores_of(scan_item[0], scan_item[1])
        return (jnp.maximum(running_max, lax.optimization_barrier(jnp.max(jnp.where(allowed, scores, NEG_FILL), -1))), None)
    indices = jnp.arange(block_count, dtype=jnp.int32)
    start_max = jnp.full((SPAN, KVH, GROUP), NEG_FILL, jnp.float32)
    row_max, _ = lax.scan(first_pass, start_max, (blocks, indices))
    row_max = jnp.maximum(row_max, sink_logit[None])

    def second_pass(running, scan_item):
        total_sum, accum = running
        scores, allowed = scores_of(scan_item[0], scan_item[1])
        probs = jnp.where(allowed, jnp.exp(scores - row_max[..., None]), 0.0)
        rounded = lax.optimization_barrier(probs.astype(jnp.bfloat16)).astype(jnp.float32)
        accum = accum + jnp.einsum('qhgk,hkd->qhgd', rounded, scan_item[0][..., head_dim:].astype(jnp.float32))
        return ((total_sum + lax.optimization_barrier(jnp.sum(probs, -1)), accum), None)
    start_sums = (jnp.zeros((SPAN, KVH, GROUP), jnp.float32), jnp.zeros((SPAN, KVH, GROUP, head_dim), jnp.float32))
    (total_sum, accum), _ = lax.scan(second_pass, start_sums, (blocks, indices))
    total_sum = total_sum + jnp.exp(sink_logit[None] - row_max)
    result = accum / total_sum[..., None]
    result = jnp.where((positions < span_count)[:, None, None, None], result, 0.0)
    return result.reshape(SPAN, KVH * GROUP * head_dim).astype(jnp.bfloat16)

def reference(queries, span_kv, cache_kv, prefix_len, span_len, sinks, out_proj, residual, norm_gain, expert_ids, expert_weights, w_gate, w_up, w_down, finished_pages, page_table):
    query_all = queries.reshape(REQS, SPAN, KVH, GROUP, HD)
    span_keys = jnp.transpose(span_kv.reshape(REQS, SPAN, KVH, 2 * HD), (0, 2, 1, 3))
    keys_all = jnp.concatenate([cache_kv, span_keys], axis=2)
    sink_logit = sinks.reshape(KVH, GROUP)

    def one_request(inputs):
        return attend_request(inputs[0], inputs[1], sink_logit, inputs[2], inputs[3])
    attention = lax.map(one_request, (query_all, keys_all, prefix_len, span_len)).reshape(TOKENS, QH * HD)
    projected = jnp.dot(attention, out_proj, preferred_element_type=jnp.float32)
    hidden_in = (residual.astype(jnp.float32) + projected).astype(jnp.bfloat16)
    widened = hidden_in.astype(jnp.float32)
    normed = (widened * lax.rsqrt(lax.optimization_barrier(jnp.mean(widened * widened, -1, keepdims=True)) + 1e-05) * norm_gain).astype(jnp.bfloat16)
    flat_ids = expert_ids.reshape(-1).astype(jnp.int32)
    assign_count = TOKENS * TOP
    ordering = jnp.argsort(flat_ids, stable=True).astype(jnp.int32)
    counts = lax.optimization_barrier(jnp.sum((flat_ids[:, None] == jnp.arange(EXPERTS, dtype=jnp.int32)[None, :]).astype(jnp.int32), 0)).astype(jnp.int32)
    offsets = (jnp.cumsum(counts) - counts).astype(jnp.int32)
    max_rows = N_REQ * N_BLK * CAP
    sorted_rows = normed[ordering // TOP]
    padded = jnp.concatenate([sorted_rows, jnp.zeros((max_rows, D), jnp.bfloat16)], 0)

    def run_expert(expert):
        first_row = offsets[expert]
        expert_rows = lax.dynamic_slice_in_dim(padded, first_row, max_rows, 0)
        gate_pre = jnp.dot(expert_rows, w_gate[expert], preferred_element_type=jnp.float32)
        up_pre = jnp.dot(expert_rows, w_up[expert], preferred_element_type=jnp.float32)
        gated = jnp.minimum(gate_pre, 7.0)
        active = ((jnp.clip(up_pre, -7.0, 7.0) + 1.0) * gated * jax.nn.sigmoid(1.702 * gated)).astype(jnp.bfloat16)
        down_rows = w_down[expert]
        combined = jnp.zeros((max_rows, D), jnp.float32)
        for part_index in range(N_HEAD):
            partial_value = jnp.dot(active[:, part_index * FF_PART:(part_index + 1) * FF_PART], down_rows[part_index * FF_PART:(part_index + 1) * FF_PART], preferred_element_type=jnp.float32)
            combined = combined + lax.optimization_barrier(partial_value.astype(jnp.bfloat16)).astype(jnp.float32)
        return combined
    expert_out = lax.map(run_expert, jnp.arange(EXPERTS, dtype=jnp.int32))
    sorted_pos = jnp.zeros((assign_count,), jnp.int32).at[ordering].set(jnp.arange(assign_count, dtype=jnp.int32))
    local_row = (sorted_pos - offsets[flat_ids]).astype(jnp.int32)
    contrib = expert_out[flat_ids, local_row].reshape(TOKENS, TOP, D)
    mixed = lax.optimization_barrier(jnp.sum(contrib * expert_weights[..., None], 1))
    layer_out = (hidden_in.astype(jnp.float32) + mixed).astype(jnp.bfloat16)
    moved_pages = jnp.zeros_like(finished_pages).at[page_table].set(finished_pages)
    return (layer_out, moved_pages)
```

```python
import math

import jax
import jax.numpy as jnp
from jax import lax
from jax.sharding import PartitionSpec as P

NEG_FILL = -1e30


def online_update(running, query_block, key_rows, allowed, score_scale):
    running_max, running_sum, running_acc = running
    head_dim = query_block.shape[-1]
    scores = (
        jnp.einsum(
            "qhgd,hkd->qhgk",
            query_block,
            key_rows[..., :head_dim],
            preferred_element_type=jnp.float32,
        )
        * score_scale
    )
    wide_mask = allowed[:, None, None, :]
    scores = jnp.where(wide_mask, scores, NEG_FILL)
    fresh_max = jnp.maximum(running_max, jnp.max(scores, -1))
    probs = jnp.where(wide_mask, jnp.exp(scores - fresh_max[..., None]), 0.0)
    factor = jnp.exp(running_max - fresh_max)
    running_sum = running_sum * factor + jnp.sum(probs, -1)
    running_acc = running_acc * factor[..., None] + jnp.einsum(
        "qhgk,hkd->qhgd",
        probs.astype(jnp.bfloat16),
        key_rows[..., head_dim:],
        preferred_element_type=jnp.float32,
    )
    return (fresh_max, running_sum, running_acc)


def sweep_cache(running, query_block, cache_rows, limit_pos, score_scale):
    kv_heads, row_count, twice_dim = cache_rows.shape
    block_len = math.gcd(512, row_count)
    block_count = row_count // block_len
    blocks = jnp.moveaxis(cache_rows.reshape(kv_heads, block_count, block_len, twice_dim), 1, 0)
    query_count = query_block.shape[0]

    def visit(state_now, scan_item):
        key_rows, block_index = scan_item
        key_pos = block_index * block_len + jnp.arange(block_len, dtype=jnp.int32)
        allowed = jnp.broadcast_to((key_pos < limit_pos)[None, :], (query_count, block_len))
        return (online_update(state_now, query_block, key_rows, allowed, score_scale), None)

    running, _ = lax.scan(visit, running, (blocks, jnp.arange(block_count, dtype=jnp.int32)))
    return running


def empty_state(row_count, kv_heads, group_size, head_dim):
    return (
        jnp.full((row_count, kv_heads, group_size), NEG_FILL, jnp.float32),
        jnp.zeros((row_count, kv_heads, group_size), jnp.float32),
        jnp.zeros((row_count, kv_heads, group_size, head_dim), jnp.float32),
    )


def finish_rows(running_max, running_sum, running_acc, sink_logit, valid_rows):
    top_logit = jnp.maximum(running_max, sink_logit[None])
    shrink = jnp.exp(running_max - top_logit)
    denominator = running_sum * shrink + jnp.exp(sink_logit[None] - top_logit)
    result = running_acc * (shrink / denominator)[..., None]
    result = jnp.where(valid_rows[:, None, None, None], result, 0.0)
    return result.reshape(result.shape[0], -1).astype(jnp.bfloat16)


def row_norm(rows, norm_gain):
    widened = rows.astype(jnp.float32)
    return (
        widened * lax.rsqrt(jnp.mean(widened * widened, -1, keepdims=True) + 1e-05) * norm_gain
    ).astype(jnp.bfloat16)


def pack_rows(table, rows, src_count, exp_local, capacity):
    packed = lax.dot_general(
        table, rows, (((0,), (0,)), ((), ())), preferred_element_type=jnp.float32
    ).astype(jnp.bfloat16)
    return packed.reshape(src_count, exp_local, capacity, -1)


def swiglu_clamped(gate_pre, up_pre):
    gated = jnp.minimum(gate_pre, 7.0)
    return ((jnp.clip(up_pre, -7.0, 7.0) + 1.0) * gated * jax.nn.sigmoid(1.702 * gated)).astype(
        jnp.bfloat16
    )


def expert_partials(arrived, w_gate, w_up, w_down):
    gate_pre = jnp.einsum("secd,edf->secf", arrived, w_gate, preferred_element_type=jnp.float32)
    up_pre = jnp.einsum("secd,edf->secf", arrived, w_up, preferred_element_type=jnp.float32)
    active = swiglu_clamped(gate_pre, up_pre)
    return jnp.einsum("secf,efd->secd", active, w_down, preferred_element_type=jnp.float32).astype(
        jnp.bfloat16
    )


def weighted_mix(back_rows, slots, expert_weights):
    tok_rows, top_k = expert_weights.shape
    picked = back_rows[slots].reshape(tok_rows, top_k, -1)
    return jnp.einsum("tk,tkd->td", expert_weights, picked.astype(jnp.float32))


def per_device(
    queries,
    span_kv,
    cache_kv,
    prefix_len,
    span_len,
    sinks,
    out_proj,
    residual,
    norm_gain,
    expert_ids,
    expert_weights,
    w_gate,
    w_up,
    w_down,
    finished_pages,
    page_table,
):
    tok_rows = queries.shape[0]
    req_local, kv_heads, block_len, twice_dim = cache_kv.shape
    head_dim = twice_dim // 2
    group_size = queries.shape[1] // (kv_heads * head_dim)
    score_scale = head_dim ** (-0.5)
    blk_count = lax.axis_size("blk")
    req_count = lax.axis_size("req")
    src_count = req_count * blk_count
    span_rows = tok_rows * blk_count // req_local
    blk_index = lax.axis_index("blk")
    own_request = blk_index * tok_rows // span_rows
    own_pos = blk_index * tok_rows % span_rows + jnp.arange(tok_rows, dtype=jnp.int32)
    sink_logit = sinks.reshape(kv_heads, group_size)
    query_block = queries.reshape(tok_rows, kv_heads, group_size, head_dim)
    own_limit = lax.dynamic_index_in_dim(span_len, own_request, 0, keepdims=False)
    valid_rows = own_pos < own_limit
    every_span = lax.all_gather(span_kv, "blk", axis=0, tiled=True)
    prefix_limit = lax.dynamic_index_in_dim(prefix_len, own_request, 0, keepdims=False)
    own_rows = lax.dynamic_index_in_dim(
        lax.all_gather(cache_kv, "blk", axis=2, tiled=True), own_request, 0, keepdims=False
    )
    running = sweep_cache(
        empty_state(tok_rows, kv_heads, group_size, head_dim),
        query_block,
        own_rows,
        prefix_limit,
        score_scale,
    )
    self_keys = jnp.transpose(every_span, (1, 0, 2))
    allowed = jnp.arange(span_rows, dtype=jnp.int32)[None, :] <= own_pos[:, None]
    running = online_update(running, query_block, self_keys, allowed, score_scale)
    attention = finish_rows(running[0], running[1], running[2], sink_logit, valid_rows)
    projected = jnp.dot(attention, out_proj, preferred_element_type=jnp.float32)
    exp_local = w_gate.shape[0]
    experts = exp_local * src_count
    top_k = expert_ids.shape[1]
    capacity = max(2, 2 * tok_rows * top_k // experts)
    flat_ids = expert_ids.reshape(-1)
    onehot = (flat_ids[:, None] == jnp.arange(experts, dtype=jnp.int32)[None, :]).astype(jnp.int32)
    ranks = jnp.sum((jnp.cumsum(onehot, 0) - onehot) * onehot, 1)
    slots = flat_ids * capacity + ranks
    table = jnp.any(
        slots.reshape(tok_rows, top_k)[:, :, None]
        == jnp.arange(experts * capacity, dtype=jnp.int32)[None, None, :],
        1,
    ).astype(jnp.bfloat16)
    head_index = lax.axis_index("head")
    column_count = residual.shape[1] // lax.axis_size("head")
    own_columns = lax.dynamic_slice_in_dim(residual, head_index * column_count, column_count, 1)
    summed = lax.psum_scatter(
        projected.astype(jnp.bfloat16), "head", scatter_dimension=1, tiled=True
    ).astype(jnp.float32)
    hidden_cols = (own_columns.astype(jnp.float32) + summed).astype(jnp.bfloat16)
    outgoing = pack_rows(table, hidden_cols, src_count, exp_local, capacity)
    arrived = lax.all_to_all(outgoing, ("req", "blk"), split_axis=0, concat_axis=0, tiled=True)
    arrived = lax.all_gather(arrived, "head", axis=3, tiled=True)
    normed = row_norm(arrived, norm_gain)
    partial_out = expert_partials(normed, w_gate, w_up, w_down)
    partial_out = lax.psum_scatter(partial_out, "head", scatter_dimension=3, tiled=True)
    returned = lax.all_to_all(partial_out, ("req", "blk"), split_axis=0, concat_axis=0, tiled=True)
    mixed = weighted_mix(returned.reshape(experts * capacity, -1), slots, expert_weights)
    layer_out = (hidden_cols.astype(jnp.float32) + mixed).astype(jnp.bfloat16)
    own_slot = lax.axis_index(("req", "blk"))
    pages_dev = finished_pages.shape[0]
    per_pair = pages_dev // src_count
    my_table = lax.dynamic_slice_in_dim(page_table, own_slot * pages_dev, pages_dev, 0)
    sort_key = my_table // pages_dev * pages_dev + jnp.arange(pages_dev, dtype=jnp.int32)
    ordering = jnp.argsort(sort_key)
    outbound = finished_pages[ordering]
    inbound = lax.all_to_all(
        outbound.reshape((src_count, per_pair) + outbound.shape[1:]),
        ("req", "blk"),
        split_axis=0,
        concat_axis=0,
        tiled=True,
    )
    inbound = inbound.reshape(finished_pages.shape)
    whole_table = page_table.reshape(src_count, pages_dev)
    marked = (
        jnp.where(whole_table // pages_dev == own_slot, 0, 1) * pages_dev
        + jnp.arange(pages_dev, dtype=jnp.int32)[None, :]
    )
    chosen = jnp.argsort(marked, axis=1)[:, :per_pair]
    arrived_slots = jnp.take_along_axis(whole_table, chosen, 1).reshape(-1) - own_slot * pages_dev
    moved_pages = inbound[jnp.argsort(arrived_slots)]
    return (layer_out, moved_pages)


def solution(mesh):
    in_specs = (
        P(("req", "blk"), "head"),
        P(("req", "blk"), "head", None),
        P("req", "head", "blk", None),
        P("req"),
        P("req"),
        P("head"),
        P("head", None),
        P(("req", "blk"), None),
        P(),
        P(("req", "blk"), None),
        P(("req", "blk"), None),
        P(("req", "blk"), None, "head"),
        P(("req", "blk"), None, "head"),
        P(("req", "blk"), "head", None),
        P(("req", "blk"), None, "head", None, None),
        P(),
    )
    out_specs = (P(("req", "blk"), "head"), P(("req", "blk"), None, "head", None, None))
    return jax.shard_map(
        per_device, mesh=mesh, in_specs=in_specs, out_specs=out_specs, check_vma=False
    )
```

```python
import math

import jax
import jax.numpy as jnp
from jax import lax
from jax.sharding import PartitionSpec as P

NEG_FILL = -1e30


def online_update(running, query_block, key_rows, allowed, score_scale):
    running_max, running_sum, running_acc = running
    head_dim = query_block.shape[-1]
    scores = (
        jnp.einsum(
            "qhgd,hkd->qhgk",
            query_block,
            key_rows[..., :head_dim],
            preferred_element_type=jnp.float32,
        )
        * score_scale
    )
    wide_mask = allowed[:, None, None, :]
    scores = jnp.where(wide_mask, scores, NEG_FILL)
    fresh_max = jnp.maximum(running_max, jnp.max(scores, -1))
    probs = jnp.where(wide_mask, jnp.exp(scores - fresh_max[..., None]), 0.0)
    factor = jnp.exp(running_max - fresh_max)
    running_sum = running_sum * factor + jnp.sum(probs, -1)
    running_acc = running_acc * factor[..., None] + jnp.einsum(
        "qhgk,hkd->qhgd",
        probs.astype(jnp.bfloat16),
        key_rows[..., head_dim:],
        preferred_element_type=jnp.float32,
    )
    return (fresh_max, running_sum, running_acc)


def sweep_cache(running, query_block, cache_rows, limit_pos, score_scale):
    kv_heads, row_count, twice_dim = cache_rows.shape
    block_len = math.gcd(512, row_count)
    block_count = row_count // block_len
    blocks = jnp.moveaxis(cache_rows.reshape(kv_heads, block_count, block_len, twice_dim), 1, 0)
    query_count = query_block.shape[0]

    def visit(state_now, scan_item):
        key_rows, block_index = scan_item
        key_pos = block_index * block_len + jnp.arange(block_len, dtype=jnp.int32)
        allowed = jnp.broadcast_to((key_pos < limit_pos)[None, :], (query_count, block_len))
        return (online_update(state_now, query_block, key_rows, allowed, score_scale), None)

    running, _ = lax.scan(visit, running, (blocks, jnp.arange(block_count, dtype=jnp.int32)))
    return running


def empty_state(row_count, kv_heads, group_size, head_dim):
    return (
        jnp.full((row_count, kv_heads, group_size), NEG_FILL, jnp.float32),
        jnp.zeros((row_count, kv_heads, group_size), jnp.float32),
        jnp.zeros((row_count, kv_heads, group_size, head_dim), jnp.float32),
    )


def finish_rows(running_max, running_sum, running_acc, sink_logit, valid_rows):
    top_logit = jnp.maximum(running_max, sink_logit[None])
    shrink = jnp.exp(running_max - top_logit)
    denominator = running_sum * shrink + jnp.exp(sink_logit[None] - top_logit)
    result = running_acc * (shrink / denominator)[..., None]
    result = jnp.where(valid_rows[:, None, None, None], result, 0.0)
    return result.reshape(result.shape[0], -1).astype(jnp.bfloat16)


def column_norm(columns, norm_gain):
    widened = columns.astype(jnp.float32)
    return (
        widened
        * lax.rsqrt(jnp.mean(widened * widened, 0, keepdims=True) + 1e-05)
        * norm_gain[:, None]
    ).astype(jnp.bfloat16)


def expert_partials_t(normed_t, w_gate, w_up, w_down):
    gate_pre = jnp.einsum("dr,df->rf", normed_t, w_gate, preferred_element_type=jnp.float32)
    up_pre = jnp.einsum("dr,df->rf", normed_t, w_up, preferred_element_type=jnp.float32)
    active = swiglu_clamped(gate_pre, up_pre)
    return jnp.einsum("rf,fd->dr", active, w_down, preferred_element_type=jnp.float32).astype(
        jnp.bfloat16
    )


def pack_rows(table, rows, src_count, exp_local, capacity):
    packed = lax.dot_general(
        table, rows, (((0,), (0,)), ((), ())), preferred_element_type=jnp.float32
    ).astype(jnp.bfloat16)
    return packed.reshape(src_count, exp_local, capacity, -1)


def swiglu_clamped(gate_pre, up_pre):
    gated = jnp.minimum(gate_pre, 7.0)
    return ((jnp.clip(up_pre, -7.0, 7.0) + 1.0) * gated * jax.nn.sigmoid(1.702 * gated)).astype(
        jnp.bfloat16
    )


def weighted_mix(back_rows, slots, expert_weights):
    tok_rows, top_k = expert_weights.shape
    picked = back_rows[slots].reshape(tok_rows, top_k, -1)
    return jnp.einsum("tk,tkd->td", expert_weights, picked.astype(jnp.float32))


def per_device(
    queries,
    span_kv,
    cache_kv,
    prefix_len,
    span_len,
    sinks,
    out_proj,
    residual,
    norm_gain,
    expert_ids,
    expert_weights,
    w_gate,
    w_up,
    w_down,
    finished_pages,
    page_table,
):
    tok_rows = queries.shape[0]
    req_local, kv_heads, block_len, twice_dim = cache_kv.shape
    head_dim = twice_dim // 2
    group_size = queries.shape[1] // (kv_heads * head_dim)
    score_scale = head_dim ** (-0.5)
    blk_count = lax.axis_size("blk")
    req_count = lax.axis_size("req")
    src_count = req_count * blk_count
    span_rows = tok_rows * blk_count // req_local
    blk_index = lax.axis_index("blk")
    own_request = blk_index * tok_rows // span_rows
    own_pos = blk_index * tok_rows % span_rows + jnp.arange(tok_rows, dtype=jnp.int32)
    sink_logit = sinks.reshape(kv_heads, group_size)
    query_block = queries.reshape(tok_rows, kv_heads, group_size, head_dim)
    own_limit = lax.dynamic_index_in_dim(span_len, own_request, 0, keepdims=False)
    valid_rows = own_pos < own_limit
    every_span = lax.all_gather(span_kv, "blk", axis=0, tiled=True)
    prefix_limit = lax.dynamic_index_in_dim(prefix_len, own_request, 0, keepdims=False)
    own_rows = lax.dynamic_index_in_dim(
        lax.all_gather(cache_kv, "blk", axis=2, tiled=True), own_request, 0, keepdims=False
    )
    running = sweep_cache(
        empty_state(tok_rows, kv_heads, group_size, head_dim),
        query_block,
        own_rows,
        prefix_limit,
        score_scale,
    )
    self_keys = jnp.transpose(every_span, (1, 0, 2))
    allowed = jnp.arange(span_rows, dtype=jnp.int32)[None, :] <= own_pos[:, None]
    running = online_update(running, query_block, self_keys, allowed, score_scale)
    attention = finish_rows(running[0], running[1], running[2], sink_logit, valid_rows)
    projected = jnp.dot(attention, out_proj, preferred_element_type=jnp.float32)
    exp_local = w_gate.shape[0]
    experts = exp_local * src_count
    top_k = expert_ids.shape[1]
    capacity = max(2, 2 * tok_rows * top_k // experts)
    flat_ids = expert_ids.reshape(-1)
    onehot = (flat_ids[:, None] == jnp.arange(experts, dtype=jnp.int32)[None, :]).astype(jnp.int32)
    ranks = jnp.sum((jnp.cumsum(onehot, 0) - onehot) * onehot, 1)
    slots = flat_ids * capacity + ranks
    table = jnp.any(
        slots.reshape(tok_rows, top_k)[:, :, None]
        == jnp.arange(experts * capacity, dtype=jnp.int32)[None, None, :],
        1,
    ).astype(jnp.bfloat16)
    head_index = lax.axis_index("head")
    column_count = residual.shape[1] // lax.axis_size("head")
    own_columns = lax.dynamic_slice_in_dim(residual, head_index * column_count, column_count, 1)
    summed = lax.psum_scatter(
        projected.astype(jnp.bfloat16), "head", scatter_dimension=1, tiled=True
    ).astype(jnp.float32)
    hidden_cols = (own_columns.astype(jnp.float32) + summed).astype(jnp.bfloat16)
    outgoing = pack_rows(table, hidden_cols, src_count, exp_local, capacity)
    arrived = lax.all_to_all(outgoing, ("req", "blk"), split_axis=0, concat_axis=0, tiled=True)
    slot_total = experts * capacity
    arrived = jnp.transpose(arrived.reshape(slot_total, column_count))
    arrived = lax.all_gather(arrived, "head", axis=0, tiled=True)
    normed = column_norm(arrived, norm_gain)
    partial_out = expert_partials_t(normed, w_gate[0], w_up[0], w_down[0])
    partial_out = lax.psum_scatter(partial_out, "head", scatter_dimension=0, tiled=True)
    partial_out = jnp.transpose(partial_out).reshape(src_count, exp_local, capacity, column_count)
    returned = lax.all_to_all(partial_out, ("req", "blk"), split_axis=0, concat_axis=0, tiled=True)
    mixed = weighted_mix(returned.reshape(experts * capacity, -1), slots, expert_weights)
    layer_out = (hidden_cols.astype(jnp.float32) + mixed).astype(jnp.bfloat16)
    own_slot = lax.axis_index(("req", "blk"))
    pages_dev = finished_pages.shape[0]
    per_pair = pages_dev // src_count
    my_table = lax.dynamic_slice_in_dim(page_table, own_slot * pages_dev, pages_dev, 0)
    sort_key = my_table // pages_dev * pages_dev + jnp.arange(pages_dev, dtype=jnp.int32)
    ordering = jnp.argsort(sort_key)
    outbound = finished_pages[ordering]
    inbound = lax.all_to_all(
        outbound.reshape((src_count, per_pair) + outbound.shape[1:]),
        ("req", "blk"),
        split_axis=0,
        concat_axis=0,
        tiled=True,
    )
    inbound = inbound.reshape(finished_pages.shape)
    whole_table = page_table.reshape(src_count, pages_dev)
    marked = (
        jnp.where(whole_table // pages_dev == own_slot, 0, 1) * pages_dev
        + jnp.arange(pages_dev, dtype=jnp.int32)[None, :]
    )
    chosen = jnp.argsort(marked, axis=1)[:, :per_pair]
    arrived_slots = jnp.take_along_axis(whole_table, chosen, 1).reshape(-1) - own_slot * pages_dev
    moved_pages = inbound[jnp.argsort(arrived_slots)]
    return (layer_out, moved_pages)


def solution(mesh):
    in_specs = (
        P(("req", "blk"), "head"),
        P(("req", "blk"), "head", None),
        P("req", "head", "blk", None),
        P("req"),
        P("req"),
        P("head"),
        P("head", None),
        P(("req", "blk"), None),
        P(),
        P(("req", "blk"), None),
        P(("req", "blk"), None),
        P(("req", "blk"), None, "head"),
        P(("req", "blk"), None, "head"),
        P(("req", "blk"), "head", None),
        P(("req", "blk"), None, "head", None, None),
        P(),
    )
    out_specs = (P(("req", "blk"), "head"), P(("req", "blk"), None, "head", None, None))
    return jax.shard_map(
        per_device, mesh=mesh, in_specs=in_specs, out_specs=out_specs, check_vma=False
    )
```

```python
import math

import jax
import jax.numpy as jnp
from jax import lax
from jax.sharding import PartitionSpec as P

NEG_FILL = -1e30


def online_update(running, query_block, key_rows, allowed, score_scale):
    running_max, running_sum, running_acc = running
    head_dim = query_block.shape[-1]
    scores = (
        jnp.einsum(
            "qhgd,hkd->qhgk",
            query_block,
            key_rows[..., :head_dim],
            preferred_element_type=jnp.float32,
        )
        * score_scale
    )
    wide_mask = allowed[:, None, None, :]
    scores = jnp.where(wide_mask, scores, NEG_FILL)
    fresh_max = jnp.maximum(running_max, jnp.max(scores, -1))
    probs = jnp.where(wide_mask, jnp.exp(scores - fresh_max[..., None]), 0.0)
    factor = jnp.exp(running_max - fresh_max)
    running_sum = running_sum * factor + jnp.sum(probs, -1)
    running_acc = running_acc * factor[..., None] + jnp.einsum(
        "qhgk,hkd->qhgd",
        probs.astype(jnp.bfloat16),
        key_rows[..., head_dim:],
        preferred_element_type=jnp.float32,
    )
    return (fresh_max, running_sum, running_acc)


def sweep_cache(running, query_block, cache_rows, limit_pos, score_scale):
    kv_heads, row_count, twice_dim = cache_rows.shape
    block_len = math.gcd(512, row_count)
    block_count = row_count // block_len
    blocks = jnp.moveaxis(cache_rows.reshape(kv_heads, block_count, block_len, twice_dim), 1, 0)
    query_count = query_block.shape[0]

    def visit(state_now, scan_item):
        key_rows, block_index = scan_item
        key_pos = block_index * block_len + jnp.arange(block_len, dtype=jnp.int32)
        allowed = jnp.broadcast_to((key_pos < limit_pos)[None, :], (query_count, block_len))
        return (online_update(state_now, query_block, key_rows, allowed, score_scale), None)

    running, _ = lax.scan(visit, running, (blocks, jnp.arange(block_count, dtype=jnp.int32)))
    return running


def masked_scores(query_block, key_rows, allowed, score_scale):
    head_dim = query_block.shape[-1]
    scores = (
        jnp.einsum(
            "qhgd,hkd->qhgk",
            query_block,
            key_rows[..., :head_dim],
            preferred_element_type=jnp.float32,
        )
        * score_scale
    )
    return jnp.where(allowed, scores, NEG_FILL)


def dense_attention(
    query_block, cache_rows, span_rows, prefix_limit, own_pos, valid_rows, sink_logit, score_scale
):
    head_dim = query_block.shape[-1]
    cache_pos = jnp.arange(cache_rows.shape[1], dtype=jnp.int32)
    cache_ok = (cache_pos < prefix_limit)[None, None, None, :]
    span_pos = jnp.arange(span_rows.shape[1], dtype=jnp.int32)
    span_ok = (span_pos[None, :] <= own_pos[:, None])[:, None, None, :]
    cache_scores = masked_scores(query_block, cache_rows, cache_ok, score_scale)
    span_scores = masked_scores(query_block, span_rows, span_ok, score_scale)
    row_max = jnp.maximum(
        jnp.maximum(jnp.max(cache_scores, -1), jnp.max(span_scores, -1)), sink_logit[None]
    )
    cache_probs = jnp.exp(cache_scores - row_max[..., None])
    span_probs = jnp.exp(span_scores - row_max[..., None])
    total = (
        jnp.sum(cache_probs, -1) + jnp.sum(span_probs, -1) + jnp.exp(sink_logit[None] - row_max)
    )
    acc = jnp.einsum(
        "qhgk,hkd->qhgd",
        cache_probs.astype(jnp.bfloat16),
        cache_rows[..., head_dim:],
        preferred_element_type=jnp.float32,
    ) + jnp.einsum(
        "qhgk,hkd->qhgd",
        span_probs.astype(jnp.bfloat16),
        span_rows[..., head_dim:],
        preferred_element_type=jnp.float32,
    )
    result = acc / total[..., None]
    result = jnp.where(valid_rows[:, None, None, None], result, 0.0)
    return result.reshape(result.shape[0], -1).astype(jnp.bfloat16)


def empty_state(row_count, kv_heads, group_size, head_dim):
    return (
        jnp.full((row_count, kv_heads, group_size), NEG_FILL, jnp.float32),
        jnp.zeros((row_count, kv_heads, group_size), jnp.float32),
        jnp.zeros((row_count, kv_heads, group_size, head_dim), jnp.float32),
    )


def finish_rows(running_max, running_sum, running_acc, sink_logit, valid_rows):
    top_logit = jnp.maximum(running_max, sink_logit[None])
    shrink = jnp.exp(running_max - top_logit)
    denominator = running_sum * shrink + jnp.exp(sink_logit[None] - top_logit)
    result = running_acc * (shrink / denominator)[..., None]
    result = jnp.where(valid_rows[:, None, None, None], result, 0.0)
    return result.reshape(result.shape[0], -1).astype(jnp.bfloat16)


def column_norm(columns, norm_gain):
    widened = columns.astype(jnp.float32)
    return (
        widened
        * lax.rsqrt(jnp.mean(widened * widened, 0, keepdims=True) + 1e-05)
        * norm_gain[:, None]
    ).astype(jnp.bfloat16)


def expert_partials_t(normed_t, w_gate, w_up, w_down):
    gate_pre = jnp.einsum("dr,df->rf", normed_t, w_gate, preferred_element_type=jnp.float32)
    up_pre = jnp.einsum("dr,df->rf", normed_t, w_up, preferred_element_type=jnp.float32)
    active = swiglu_clamped(gate_pre, up_pre)
    return jnp.einsum("rf,fd->dr", active, w_down, preferred_element_type=jnp.float32).astype(
        jnp.bfloat16
    )


def pack_rows(table, rows, src_count, exp_local, capacity):
    packed = lax.dot_general(
        table, rows, (((0,), (0,)), ((), ())), preferred_element_type=jnp.float32
    ).astype(jnp.bfloat16)
    return packed.reshape(src_count, exp_local, capacity, -1)


def swiglu_clamped(gate_pre, up_pre):
    gated = jnp.minimum(gate_pre, 7.0)
    return ((jnp.clip(up_pre, -7.0, 7.0) + 1.0) * gated * jax.nn.sigmoid(1.702 * gated)).astype(
        jnp.bfloat16
    )


def weighted_mix(back_rows, slots, expert_weights):
    tok_rows, top_k = expert_weights.shape
    picked = back_rows[slots].reshape(tok_rows, top_k, -1)
    return jnp.einsum("tk,tkd->td", expert_weights, picked.astype(jnp.float32))


def per_device(
    queries,
    span_kv,
    cache_kv,
    prefix_len,
    span_len,
    sinks,
    out_proj,
    residual,
    norm_gain,
    expert_ids,
    expert_weights,
    w_gate,
    w_up,
    w_down,
    finished_pages,
    page_table,
):
    tok_rows = queries.shape[0]
    req_local, kv_heads, block_len, twice_dim = cache_kv.shape
    head_dim = twice_dim // 2
    group_size = queries.shape[1] // (kv_heads * head_dim)
    score_scale = head_dim ** (-0.5)
    blk_count = lax.axis_size("blk")
    req_count = lax.axis_size("req")
    src_count = req_count * blk_count
    span_rows = tok_rows * blk_count // req_local
    blk_index = lax.axis_index("blk")
    own_request = blk_index * tok_rows // span_rows
    own_pos = blk_index * tok_rows % span_rows + jnp.arange(tok_rows, dtype=jnp.int32)
    sink_logit = sinks.reshape(kv_heads, group_size)
    query_block = queries.reshape(tok_rows, kv_heads, group_size, head_dim)
    own_limit = lax.dynamic_index_in_dim(span_len, own_request, 0, keepdims=False)
    valid_rows = own_pos < own_limit
    every_span = lax.all_gather(span_kv, "blk", axis=0, tiled=True)
    prefix_limit = lax.dynamic_index_in_dim(prefix_len, own_request, 0, keepdims=False)
    own_rows = lax.dynamic_index_in_dim(
        lax.all_gather(cache_kv, "blk", axis=2, tiled=True), own_request, 0, keepdims=False
    )
    self_keys = jnp.transpose(every_span, (1, 0, 2))
    attention = dense_attention(
        query_block, own_rows, self_keys, prefix_limit, own_pos, valid_rows, sink_logit, score_scale
    )
    projected = jnp.dot(attention, out_proj, preferred_element_type=jnp.float32)
    exp_local = w_gate.shape[0]
    experts = exp_local * src_count
    top_k = expert_ids.shape[1]
    capacity = max(2, 2 * tok_rows * top_k // experts)
    flat_ids = expert_ids.reshape(-1)
    onehot = (flat_ids[:, None] == jnp.arange(experts, dtype=jnp.int32)[None, :]).astype(jnp.int32)
    ranks = jnp.sum((jnp.cumsum(onehot, 0) - onehot) * onehot, 1)
    slots = flat_ids * capacity + ranks
    table = jnp.any(
        slots.reshape(tok_rows, top_k)[:, :, None]
        == jnp.arange(experts * capacity, dtype=jnp.int32)[None, None, :],
        1,
    ).astype(jnp.bfloat16)
    head_index = lax.axis_index("head")
    column_count = residual.shape[1] // lax.axis_size("head")
    own_columns = lax.dynamic_slice_in_dim(residual, head_index * column_count, column_count, 1)
    summed = lax.psum_scatter(
        projected.astype(jnp.bfloat16), "head", scatter_dimension=1, tiled=True
    ).astype(jnp.float32)
    hidden_cols = (own_columns.astype(jnp.float32) + summed).astype(jnp.bfloat16)
    outgoing = pack_rows(table, hidden_cols, src_count, exp_local, capacity)
    arrived = lax.all_to_all(outgoing, ("req", "blk"), split_axis=0, concat_axis=0, tiled=True)
    slot_total = experts * capacity
    arrived = jnp.transpose(arrived.reshape(slot_total, column_count))
    arrived = lax.all_gather(arrived, "head", axis=0, tiled=True)
    normed = column_norm(arrived, norm_gain)
    partial_out = expert_partials_t(normed, w_gate[0], w_up[0], w_down[0])
    partial_out = lax.psum_scatter(partial_out, "head", scatter_dimension=0, tiled=True)
    partial_out = jnp.transpose(partial_out).reshape(src_count, exp_local, capacity, column_count)
    returned = lax.all_to_all(partial_out, ("req", "blk"), split_axis=0, concat_axis=0, tiled=True)
    mixed = weighted_mix(returned.reshape(experts * capacity, -1), slots, expert_weights)
    layer_out = (hidden_cols.astype(jnp.float32) + mixed).astype(jnp.bfloat16)
    own_slot = lax.axis_index(("req", "blk"))
    pages_dev = finished_pages.shape[0]
    per_pair = pages_dev // src_count
    my_table = lax.dynamic_slice_in_dim(page_table, own_slot * pages_dev, pages_dev, 0)
    sort_key = my_table // pages_dev * pages_dev + jnp.arange(pages_dev, dtype=jnp.int32)
    ordering = jnp.argsort(sort_key)
    outbound = finished_pages[ordering]
    inbound = lax.all_to_all(
        outbound.reshape((src_count, per_pair) + outbound.shape[1:]),
        ("req", "blk"),
        split_axis=0,
        concat_axis=0,
        tiled=True,
    )
    inbound = inbound.reshape(finished_pages.shape)
    whole_table = page_table.reshape(src_count, pages_dev)
    marked = (
        jnp.where(whole_table // pages_dev == own_slot, 0, 1) * pages_dev
        + jnp.arange(pages_dev, dtype=jnp.int32)[None, :]
    )
    chosen = jnp.argsort(marked, axis=1)[:, :per_pair]
    arrived_slots = jnp.take_along_axis(whole_table, chosen, 1).reshape(-1) - own_slot * pages_dev
    moved_pages = inbound[jnp.argsort(arrived_slots)]
    return (layer_out, moved_pages)


def solution(mesh):
    in_specs = (
        P(("req", "blk"), "head"),
        P(("req", "blk"), "head", None),
        P("req", "head", "blk", None),
        P("req"),
        P("req"),
        P("head"),
        P("head", None),
        P(("req", "blk"), None),
        P(),
        P(("req", "blk"), None),
        P(("req", "blk"), None),
        P(("req", "blk"), None, "head"),
        P(("req", "blk"), None, "head"),
        P(("req", "blk"), "head", None),
        P(("req", "blk"), None, "head", None, None),
        P(),
    )
    out_specs = (P(("req", "blk"), "head"), P(("req", "blk"), None, "head", None, None))
    return jax.shard_map(
        per_device, mesh=mesh, in_specs=in_specs, out_specs=out_specs, check_vma=False
    )
```

```python
import math

import jax
import jax.numpy as jnp
from jax import lax
from jax.sharding import PartitionSpec as P

NEG_FILL = -1e30


def online_update(running, query_block, key_rows, allowed, score_scale):
    running_max, running_sum, running_acc = running
    head_dim = query_block.shape[-1]
    scores = (
        jnp.einsum(
            "qhgd,hkd->qhgk",
            query_block,
            key_rows[..., :head_dim],
            preferred_element_type=jnp.float32,
        )
        * score_scale
    )
    wide_mask = allowed[:, None, None, :]
    scores = jnp.where(wide_mask, scores, NEG_FILL)
    fresh_max = jnp.maximum(running_max, jnp.max(scores, -1))
    probs = jnp.where(wide_mask, jnp.exp(scores - fresh_max[..., None]), 0.0)
    factor = jnp.exp(running_max - fresh_max)
    running_sum = running_sum * factor + jnp.sum(probs, -1)
    running_acc = running_acc * factor[..., None] + jnp.einsum(
        "qhgk,hkd->qhgd",
        probs.astype(jnp.bfloat16),
        key_rows[..., head_dim:],
        preferred_element_type=jnp.float32,
    )
    return (fresh_max, running_sum, running_acc)


def sweep_cache(running, query_block, cache_rows, limit_pos, score_scale):
    kv_heads, row_count, twice_dim = cache_rows.shape
    block_len = math.gcd(512, row_count)
    block_count = row_count // block_len
    blocks = jnp.moveaxis(cache_rows.reshape(kv_heads, block_count, block_len, twice_dim), 1, 0)
    query_count = query_block.shape[0]

    def visit(state_now, scan_item):
        key_rows, block_index = scan_item
        key_pos = block_index * block_len + jnp.arange(block_len, dtype=jnp.int32)
        allowed = jnp.broadcast_to((key_pos < limit_pos)[None, :], (query_count, block_len))
        return (online_update(state_now, query_block, key_rows, allowed, score_scale), None)

    running, _ = lax.scan(visit, running, (blocks, jnp.arange(block_count, dtype=jnp.int32)))
    return running


def masked_scores(query_block, key_rows, allowed, score_scale):
    head_dim = query_block.shape[-1]
    scores = (
        jnp.einsum(
            "qhgd,hkd->qhgk",
            query_block,
            key_rows[..., :head_dim],
            preferred_element_type=jnp.float32,
        )
        * score_scale
    )
    return jnp.where(allowed, scores, NEG_FILL)


def dense_attention(
    query_block, cache_rows, span_rows, prefix_limit, own_pos, valid_rows, sink_logit, score_scale
):
    head_dim = query_block.shape[-1]
    cache_pos = jnp.arange(cache_rows.shape[1], dtype=jnp.int32)
    cache_ok = (cache_pos < prefix_limit)[None, None, None, :]
    span_pos = jnp.arange(span_rows.shape[1], dtype=jnp.int32)
    span_ok = (span_pos[None, :] <= own_pos[:, None])[:, None, None, :]
    cache_scores = masked_scores(query_block, cache_rows, cache_ok, score_scale)
    span_scores = masked_scores(query_block, span_rows, span_ok, score_scale)
    row_max = jnp.maximum(
        jnp.maximum(jnp.max(cache_scores, -1), jnp.max(span_scores, -1)), sink_logit[None]
    )
    cache_probs = jnp.exp(cache_scores - row_max[..., None])
    span_probs = jnp.exp(span_scores - row_max[..., None])
    total = (
        jnp.sum(cache_probs, -1) + jnp.sum(span_probs, -1) + jnp.exp(sink_logit[None] - row_max)
    )
    acc = jnp.einsum(
        "qhgk,hkd->qhgd",
        cache_probs.astype(jnp.bfloat16),
        cache_rows[..., head_dim:],
        preferred_element_type=jnp.float32,
    ) + jnp.einsum(
        "qhgk,hkd->qhgd",
        span_probs.astype(jnp.bfloat16),
        span_rows[..., head_dim:],
        preferred_element_type=jnp.float32,
    )
    result = acc / total[..., None]
    result = jnp.where(valid_rows[:, None, None, None], result, 0.0)
    return result.reshape(result.shape[0], -1).astype(jnp.bfloat16)


def empty_state(row_count, kv_heads, group_size, head_dim):
    return (
        jnp.full((row_count, kv_heads, group_size), NEG_FILL, jnp.float32),
        jnp.zeros((row_count, kv_heads, group_size), jnp.float32),
        jnp.zeros((row_count, kv_heads, group_size, head_dim), jnp.float32),
    )


def finish_rows(running_max, running_sum, running_acc, sink_logit, valid_rows):
    top_logit = jnp.maximum(running_max, sink_logit[None])
    shrink = jnp.exp(running_max - top_logit)
    denominator = running_sum * shrink + jnp.exp(sink_logit[None] - top_logit)
    result = running_acc * (shrink / denominator)[..., None]
    result = jnp.where(valid_rows[:, None, None, None], result, 0.0)
    return result.reshape(result.shape[0], -1).astype(jnp.bfloat16)


def column_norm(columns, norm_gain):
    widened = columns.astype(jnp.float32)
    return (
        widened
        * lax.rsqrt(jnp.mean(widened * widened, 0, keepdims=True) + 1e-05)
        * norm_gain[:, None]
    ).astype(jnp.bfloat16)


def expert_partials_t(normed_t, w_gate, w_up, w_down):
    gate_pre = jnp.einsum("dr,df->rf", normed_t, w_gate, preferred_element_type=jnp.float32)
    up_pre = jnp.einsum("dr,df->rf", normed_t, w_up, preferred_element_type=jnp.float32)
    active = swiglu_clamped(gate_pre, up_pre)
    return jnp.einsum("rf,fd->dr", active, w_down, preferred_element_type=jnp.float32).astype(
        jnp.bfloat16
    )


def pack_rows(table, rows, src_count, exp_local, capacity):
    packed = lax.dot_general(
        table, rows, (((0,), (0,)), ((), ())), preferred_element_type=jnp.float32
    ).astype(jnp.bfloat16)
    return packed.reshape(src_count, exp_local, capacity, -1)


def swiglu_clamped(gate_pre, up_pre):
    gated = jnp.minimum(gate_pre, 7.0)
    return ((jnp.clip(up_pre, -7.0, 7.0) + 1.0) * gated * jax.nn.sigmoid(1.702 * gated)).astype(
        jnp.bfloat16
    )


def weighted_mix(back_rows, slots, expert_weights):
    tok_rows, top_k = expert_weights.shape
    picked = back_rows[slots].reshape(tok_rows, top_k, -1)
    return jnp.einsum("tk,tkd->td", expert_weights, picked.astype(jnp.float32))


def per_device(
    queries,
    span_kv,
    cache_kv,
    prefix_len,
    span_len,
    sinks,
    out_proj,
    residual,
    norm_gain,
    expert_ids,
    expert_weights,
    w_gate,
    w_up,
    w_down,
    finished_pages,
    page_table,
):
    tok_rows = queries.shape[0]
    req_local, kv_heads, block_len, twice_dim = cache_kv.shape
    head_dim = twice_dim // 2
    group_size = queries.shape[1] // (kv_heads * head_dim)
    score_scale = head_dim ** (-0.5)
    blk_count = lax.axis_size("blk")
    req_count = lax.axis_size("req")
    src_count = req_count * blk_count
    span_rows = tok_rows * blk_count // req_local
    blk_index = lax.axis_index("blk")
    own_request = blk_index * tok_rows // span_rows
    own_pos = blk_index * tok_rows % span_rows + jnp.arange(tok_rows, dtype=jnp.int32)
    sink_logit = sinks.reshape(kv_heads, group_size)
    query_block = queries.reshape(tok_rows, kv_heads, group_size, head_dim)
    own_limit = lax.dynamic_index_in_dim(span_len, own_request, 0, keepdims=False)
    valid_rows = own_pos < own_limit
    every_span = lax.all_gather(span_kv, "blk", axis=0, tiled=True)
    prefix_limit = lax.dynamic_index_in_dim(prefix_len, own_request, 0, keepdims=False)
    own_rows = lax.dynamic_index_in_dim(
        lax.all_gather(cache_kv, "blk", axis=2, tiled=True), own_request, 0, keepdims=False
    )
    self_keys = jnp.transpose(every_span, (1, 0, 2))
    attention = dense_attention(
        query_block, own_rows, self_keys, prefix_limit, own_pos, valid_rows, sink_logit, score_scale
    )
    projected = jnp.dot(attention, out_proj, preferred_element_type=jnp.float32)
    exp_local = w_gate.shape[0]
    experts = exp_local * src_count
    top_k = expert_ids.shape[1]
    capacity = max(2, 2 * tok_rows * top_k // experts)
    flat_ids = expert_ids.reshape(-1)
    onehot = (flat_ids[:, None] == jnp.arange(experts, dtype=jnp.int32)[None, :]).astype(jnp.int32)
    ranks = jnp.sum((jnp.cumsum(onehot, 0) - onehot) * onehot, 1)
    slots = flat_ids * capacity + ranks
    table = jnp.any(
        slots.reshape(tok_rows, top_k)[:, :, None]
        == jnp.arange(experts * capacity, dtype=jnp.int32)[None, None, :],
        1,
    ).astype(jnp.bfloat16)
    head_index = lax.axis_index("head")
    column_count = residual.shape[1] // lax.axis_size("head")
    own_columns = lax.dynamic_slice_in_dim(residual, head_index * column_count, column_count, 1)
    head_count = lax.axis_size("head")
    pieces = jnp.transpose(
        projected.astype(jnp.bfloat16).reshape(tok_rows, head_count, column_count), (1, 0, 2)
    )
    pieces = lax.all_to_all(pieces, "head", split_axis=0, concat_axis=0, tiled=True)
    summed = jnp.sum(pieces.astype(jnp.float32), 0)
    hidden_cols = (own_columns.astype(jnp.float32) + summed).astype(jnp.bfloat16)
    outgoing = pack_rows(table, hidden_cols, src_count, exp_local, capacity)
    arrived = lax.all_to_all(outgoing, ("req", "blk"), split_axis=0, concat_axis=0, tiled=True)
    slot_total = experts * capacity
    arrived = jnp.transpose(arrived.reshape(slot_total, column_count))
    arrived = lax.all_gather(arrived, "head", axis=0, tiled=True)
    normed = column_norm(arrived, norm_gain)
    partial_out = expert_partials_t(normed, w_gate[0], w_up[0], w_down[0])
    partial_out = lax.psum_scatter(partial_out, "head", scatter_dimension=0, tiled=True)
    partial_out = jnp.transpose(partial_out).reshape(src_count, exp_local, capacity, column_count)
    returned = lax.all_to_all(partial_out, ("req", "blk"), split_axis=0, concat_axis=0, tiled=True)
    mixed = weighted_mix(returned.reshape(experts * capacity, -1), slots, expert_weights)
    layer_out = (hidden_cols.astype(jnp.float32) + mixed).astype(jnp.bfloat16)
    own_slot = lax.axis_index(("req", "blk"))
    pages_dev = finished_pages.shape[0]
    per_pair = pages_dev // src_count
    my_table = lax.dynamic_slice_in_dim(page_table, own_slot * pages_dev, pages_dev, 0)
    sort_key = my_table // pages_dev * pages_dev + jnp.arange(pages_dev, dtype=jnp.int32)
    ordering = jnp.argsort(sort_key)
    outbound = finished_pages[ordering]
    inbound = lax.all_to_all(
        outbound.reshape((src_count, per_pair) + outbound.shape[1:]),
        ("req", "blk"),
        split_axis=0,
        concat_axis=0,
        tiled=True,
    )
    inbound = inbound.reshape(finished_pages.shape)
    whole_table = page_table.reshape(src_count, pages_dev)
    marked = (
        jnp.where(whole_table // pages_dev == own_slot, 0, 1) * pages_dev
        + jnp.arange(pages_dev, dtype=jnp.int32)[None, :]
    )
    chosen = jnp.argsort(marked, axis=1)[:, :per_pair]
    arrived_slots = jnp.take_along_axis(whole_table, chosen, 1).reshape(-1) - own_slot * pages_dev
    moved_pages = inbound[jnp.argsort(arrived_slots)]
    return (layer_out, moved_pages)


def solution(mesh):
    in_specs = (
        P(("req", "blk"), "head"),
        P(("req", "blk"), "head", None),
        P("req", "head", "blk", None),
        P("req"),
        P("req"),
        P("head"),
        P("head", None),
        P(("req", "blk"), None),
        P(),
        P(("req", "blk"), None),
        P(("req", "blk"), None),
        P(("req", "blk"), None, "head"),
        P(("req", "blk"), None, "head"),
        P(("req", "blk"), "head", None),
        P(("req", "blk"), None, "head", None, None),
        P(),
    )
    out_specs = (P(("req", "blk"), "head"), P(("req", "blk"), None, "head", None, None))
    return jax.shard_map(
        per_device, mesh=mesh, in_specs=in_specs, out_specs=out_specs, check_vma=False
    )
```

```python
import math

import jax
import jax.numpy as jnp
from jax import lax
from jax.sharding import PartitionSpec as P

NEG_FILL = -1e30


def online_update(running, query_block, key_rows, allowed, score_scale):
    running_max, running_sum, running_acc = running
    head_dim = query_block.shape[-1]
    scores = (
        jnp.einsum(
            "qhgd,hkd->qhgk",
            query_block,
            key_rows[..., :head_dim],
            preferred_element_type=jnp.float32,
        )
        * score_scale
    )
    wide_mask = allowed[:, None, None, :]
    scores = jnp.where(wide_mask, scores, NEG_FILL)
    fresh_max = jnp.maximum(running_max, jnp.max(scores, -1))
    probs = jnp.where(wide_mask, jnp.exp(scores - fresh_max[..., None]), 0.0)
    factor = jnp.exp(running_max - fresh_max)
    running_sum = running_sum * factor + jnp.sum(probs, -1)
    running_acc = running_acc * factor[..., None] + jnp.einsum(
        "qhgk,hkd->qhgd",
        probs.astype(jnp.bfloat16),
        key_rows[..., head_dim:],
        preferred_element_type=jnp.float32,
    )
    return (fresh_max, running_sum, running_acc)


def sweep_cache(running, query_block, cache_rows, limit_pos, score_scale):
    kv_heads, row_count, twice_dim = cache_rows.shape
    block_len = math.gcd(512, row_count)
    block_count = row_count // block_len
    blocks = jnp.moveaxis(cache_rows.reshape(kv_heads, block_count, block_len, twice_dim), 1, 0)
    query_count = query_block.shape[0]

    def visit(state_now, scan_item):
        key_rows, block_index = scan_item
        key_pos = block_index * block_len + jnp.arange(block_len, dtype=jnp.int32)
        allowed = jnp.broadcast_to((key_pos < limit_pos)[None, :], (query_count, block_len))
        return (online_update(state_now, query_block, key_rows, allowed, score_scale), None)

    running, _ = lax.scan(visit, running, (blocks, jnp.arange(block_count, dtype=jnp.int32)))
    return running


def masked_scores(query_block, key_rows, allowed, score_scale):
    head_dim = query_block.shape[-1]
    scores = (
        jnp.einsum(
            "qhgd,hkd->qhgk",
            query_block,
            key_rows[..., :head_dim],
            preferred_element_type=jnp.float32,
        )
        * score_scale
    )
    return jnp.where(allowed, scores, NEG_FILL)


def dense_attention(
    query_block,
    cache_rows,
    span_rows,
    cache_pos,
    span_pos,
    prefix_limit,
    own_pos,
    valid_rows,
    sink_logit,
    score_scale,
):
    head_dim = query_block.shape[-1]
    cache_ok = (cache_pos < prefix_limit)[None, None, None, :]
    span_ok = (span_pos[None, :] <= own_pos[:, None])[:, None, None, :]
    cache_scores = masked_scores(query_block, cache_rows, cache_ok, score_scale)
    span_scores = masked_scores(query_block, span_rows, span_ok, score_scale)
    row_max = jnp.maximum(
        jnp.maximum(jnp.max(cache_scores, -1), jnp.max(span_scores, -1)), sink_logit[None]
    )
    cache_probs = jnp.exp(cache_scores - row_max[..., None])
    span_probs = jnp.exp(span_scores - row_max[..., None])
    total = (
        jnp.sum(cache_probs, -1) + jnp.sum(span_probs, -1) + jnp.exp(sink_logit[None] - row_max)
    )
    acc = jnp.einsum(
        "qhgk,hkd->qhgd",
        cache_probs.astype(jnp.bfloat16),
        cache_rows[..., head_dim:],
        preferred_element_type=jnp.float32,
    ) + jnp.einsum(
        "qhgk,hkd->qhgd",
        span_probs.astype(jnp.bfloat16),
        span_rows[..., head_dim:],
        preferred_element_type=jnp.float32,
    )
    result = acc / total[..., None]
    result = jnp.where(valid_rows[:, None, None, None], result, 0.0)
    return result.reshape(result.shape[0], -1).astype(jnp.bfloat16)


def empty_state(row_count, kv_heads, group_size, head_dim):
    return (
        jnp.full((row_count, kv_heads, group_size), NEG_FILL, jnp.float32),
        jnp.zeros((row_count, kv_heads, group_size), jnp.float32),
        jnp.zeros((row_count, kv_heads, group_size, head_dim), jnp.float32),
    )


def finish_rows(running_max, running_sum, running_acc, sink_logit, valid_rows):
    top_logit = jnp.maximum(running_max, sink_logit[None])
    shrink = jnp.exp(running_max - top_logit)
    denominator = running_sum * shrink + jnp.exp(sink_logit[None] - top_logit)
    result = running_acc * (shrink / denominator)[..., None]
    result = jnp.where(valid_rows[:, None, None, None], result, 0.0)
    return result.reshape(result.shape[0], -1).astype(jnp.bfloat16)


def column_norm(columns, norm_gain):
    widened = columns.astype(jnp.float32)
    return (
        widened
        * lax.rsqrt(jnp.mean(widened * widened, 0, keepdims=True) + 1e-05)
        * norm_gain[:, None]
    ).astype(jnp.bfloat16)


def expert_partials_t(normed_t, w_gate, w_up, w_down):
    gate_pre = jnp.einsum("dr,df->rf", normed_t, w_gate, preferred_element_type=jnp.float32)
    up_pre = jnp.einsum("dr,df->rf", normed_t, w_up, preferred_element_type=jnp.float32)
    active = swiglu_clamped(gate_pre, up_pre)
    return jnp.einsum("rf,fd->dr", active, w_down, preferred_element_type=jnp.float32).astype(
        jnp.bfloat16
    )


def pack_rows(table, rows, src_count, exp_local, capacity):
    packed = lax.dot_general(
        table, rows, (((0,), (0,)), ((), ())), preferred_element_type=jnp.float32
    ).astype(jnp.bfloat16)
    return packed.reshape(src_count, exp_local, capacity, -1)


def swiglu_clamped(gate_pre, up_pre):
    gated = jnp.minimum(gate_pre, 7.0)
    return ((jnp.clip(up_pre, -7.0, 7.0) + 1.0) * gated * jax.nn.sigmoid(1.702 * gated)).astype(
        jnp.bfloat16
    )


def weighted_mix(back_rows, slots, expert_weights):
    tok_rows, top_k = expert_weights.shape
    picked = back_rows[slots].reshape(tok_rows, top_k, -1)
    return jnp.einsum("tk,tkd->td", expert_weights, picked.astype(jnp.float32))


def per_device(
    queries,
    span_kv,
    cache_kv,
    prefix_len,
    span_len,
    sinks,
    out_proj,
    residual,
    norm_gain,
    expert_ids,
    expert_weights,
    w_gate,
    w_up,
    w_down,
    finished_pages,
    page_table,
):
    tok_rows = queries.shape[0]
    req_local, kv_heads, block_len, twice_dim = cache_kv.shape
    head_dim = twice_dim // 2
    group_size = queries.shape[1] // (kv_heads * head_dim)
    score_scale = head_dim ** (-0.5)
    blk_count = lax.axis_size("blk")
    req_count = lax.axis_size("req")
    src_count = req_count * blk_count
    span_rows = tok_rows * blk_count // req_local
    blk_index = lax.axis_index("blk")
    own_request = blk_index * tok_rows // span_rows
    own_pos = blk_index * tok_rows % span_rows + jnp.arange(tok_rows, dtype=jnp.int32)
    sink_logit = sinks.reshape(kv_heads, group_size)
    query_block = queries.reshape(tok_rows, kv_heads, group_size, head_dim)
    own_limit = lax.dynamic_index_in_dim(span_len, own_request, 0, keepdims=False)
    valid_rows = own_pos < own_limit
    prefix_limit = lax.dynamic_index_in_dim(prefix_len, own_request, 0, keepdims=False)
    own_cache = lax.dynamic_index_in_dim(cache_kv, own_request, 0, keepdims=False)
    payload = jnp.concatenate([own_cache, jnp.transpose(span_kv, (1, 0, 2))], 1)
    pieces = [payload]
    sources = [blk_index]
    for shift in range(1, blk_count):
        ring = [(i, (i + shift) % blk_count) for i in range(blk_count)]
        pieces.append(lax.ppermute(payload, "blk", ring))
        sources.append((blk_index - shift) % blk_count)
    cache_rows = jnp.concatenate([piece[:, :block_len] for piece in pieces], 1)
    span_keys = jnp.concatenate([piece[:, block_len:] for piece in pieces], 1)
    local_cache = jnp.arange(block_len, dtype=jnp.int32)
    local_span = jnp.arange(tok_rows, dtype=jnp.int32)
    cache_pos = jnp.concatenate([source * block_len + local_cache for source in sources])
    span_pos = jnp.concatenate([source * tok_rows + local_span for source in sources])
    attention = dense_attention(
        query_block,
        cache_rows,
        span_keys,
        cache_pos,
        span_pos,
        prefix_limit,
        own_pos,
        valid_rows,
        sink_logit,
        score_scale,
    )
    projected = jnp.dot(attention, out_proj, preferred_element_type=jnp.float32)
    exp_local = w_gate.shape[0]
    experts = exp_local * src_count
    top_k = expert_ids.shape[1]
    capacity = max(2, 2 * tok_rows * top_k // experts)
    flat_ids = expert_ids.reshape(-1)
    onehot = (flat_ids[:, None] == jnp.arange(experts, dtype=jnp.int32)[None, :]).astype(jnp.int32)
    ranks = jnp.sum((jnp.cumsum(onehot, 0) - onehot) * onehot, 1)
    slots = flat_ids * capacity + ranks
    table = jnp.any(
        slots.reshape(tok_rows, top_k)[:, :, None]
        == jnp.arange(experts * capacity, dtype=jnp.int32)[None, None, :],
        1,
    ).astype(jnp.bfloat16)
    head_index = lax.axis_index("head")
    column_count = residual.shape[1] // lax.axis_size("head")
    own_columns = lax.dynamic_slice_in_dim(residual, head_index * column_count, column_count, 1)
    head_count = lax.axis_size("head")
    pieces = jnp.transpose(
        projected.astype(jnp.bfloat16).reshape(tok_rows, head_count, column_count), (1, 0, 2)
    )
    pieces = lax.all_to_all(pieces, "head", split_axis=0, concat_axis=0, tiled=True)
    summed = jnp.sum(pieces.astype(jnp.float32), 0)
    hidden_cols = (own_columns.astype(jnp.float32) + summed).astype(jnp.bfloat16)
    outgoing = pack_rows(table, hidden_cols, src_count, exp_local, capacity)
    arrived = lax.all_to_all(outgoing, ("req", "blk"), split_axis=0, concat_axis=0, tiled=True)
    slot_total = experts * capacity
    arrived = jnp.transpose(arrived.reshape(slot_total, column_count))
    arrived = lax.all_gather(arrived, "head", axis=0, tiled=True)
    normed = column_norm(arrived, norm_gain)
    partial_out = expert_partials_t(normed, w_gate[0], w_up[0], w_down[0])
    partial_out = lax.psum_scatter(partial_out, "head", scatter_dimension=0, tiled=True)
    partial_out = jnp.transpose(partial_out).reshape(src_count, exp_local, capacity, column_count)
    returned = lax.all_to_all(partial_out, ("req", "blk"), split_axis=0, concat_axis=0, tiled=True)
    mixed = weighted_mix(returned.reshape(experts * capacity, -1), slots, expert_weights)
    layer_out = (hidden_cols.astype(jnp.float32) + mixed).astype(jnp.bfloat16)
    own_slot = lax.axis_index(("req", "blk"))
    pages_dev = finished_pages.shape[0]
    per_pair = pages_dev // src_count
    my_table = lax.dynamic_slice_in_dim(page_table, own_slot * pages_dev, pages_dev, 0)
    sort_key = my_table // pages_dev * pages_dev + jnp.arange(pages_dev, dtype=jnp.int32)
    ordering = jnp.argsort(sort_key)
    outbound = finished_pages[ordering]
    inbound = lax.all_to_all(
        outbound.reshape((src_count, per_pair) + outbound.shape[1:]),
        ("req", "blk"),
        split_axis=0,
        concat_axis=0,
        tiled=True,
    )
    inbound = inbound.reshape(finished_pages.shape)
    whole_table = page_table.reshape(src_count, pages_dev)
    marked = (
        jnp.where(whole_table // pages_dev == own_slot, 0, 1) * pages_dev
        + jnp.arange(pages_dev, dtype=jnp.int32)[None, :]
    )
    chosen = jnp.argsort(marked, axis=1)[:, :per_pair]
    arrived_slots = jnp.take_along_axis(whole_table, chosen, 1).reshape(-1) - own_slot * pages_dev
    moved_pages = inbound[jnp.argsort(arrived_slots)]
    return (layer_out, moved_pages)


def solution(mesh):
    in_specs = (
        P(("req", "blk"), "head"),
        P(("req", "blk"), "head", None),
        P("req", "head", "blk", None),
        P("req"),
        P("req"),
        P("head"),
        P("head", None),
        P(("req", "blk"), None),
        P(),
        P(("req", "blk"), None),
        P(("req", "blk"), None),
        P(("req", "blk"), None, "head"),
        P(("req", "blk"), None, "head"),
        P(("req", "blk"), "head", None),
        P(("req", "blk"), None, "head", None, None),
        P(),
    )
    out_specs = (P(("req", "blk"), "head"), P(("req", "blk"), None, "head", None, None))
    return jax.shard_map(
        per_device, mesh=mesh, in_specs=in_specs, out_specs=out_specs, check_vma=False
    )
```

```python
import math

import jax
import jax.numpy as jnp
from jax import lax
from jax.sharding import PartitionSpec as P

NEG_FILL = -1e30


def online_update(running, query_block, key_rows, allowed, score_scale):
    running_max, running_sum, running_acc = running
    head_dim = query_block.shape[-1]
    scores = (
        jnp.einsum(
            "qhgd,hkd->qhgk",
            query_block,
            key_rows[..., :head_dim],
            preferred_element_type=jnp.float32,
        )
        * score_scale
    )
    wide_mask = allowed[:, None, None, :]
    scores = jnp.where(wide_mask, scores, NEG_FILL)
    fresh_max = jnp.maximum(running_max, jnp.max(scores, -1))
    probs = jnp.where(wide_mask, jnp.exp(scores - fresh_max[..., None]), 0.0)
    factor = jnp.exp(running_max - fresh_max)
    running_sum = running_sum * factor + jnp.sum(probs, -1)
    running_acc = running_acc * factor[..., None] + jnp.einsum(
        "qhgk,hkd->qhgd",
        probs.astype(jnp.bfloat16),
        key_rows[..., head_dim:],
        preferred_element_type=jnp.float32,
    )
    return (fresh_max, running_sum, running_acc)


def sweep_cache(running, query_block, cache_rows, limit_pos, score_scale):
    kv_heads, row_count, twice_dim = cache_rows.shape
    block_len = math.gcd(512, row_count)
    block_count = row_count // block_len
    blocks = jnp.moveaxis(cache_rows.reshape(kv_heads, block_count, block_len, twice_dim), 1, 0)
    query_count = query_block.shape[0]

    def visit(state_now, scan_item):
        key_rows, block_index = scan_item
        key_pos = block_index * block_len + jnp.arange(block_len, dtype=jnp.int32)
        allowed = jnp.broadcast_to((key_pos < limit_pos)[None, :], (query_count, block_len))
        return (online_update(state_now, query_block, key_rows, allowed, score_scale), None)

    running, _ = lax.scan(visit, running, (blocks, jnp.arange(block_count, dtype=jnp.int32)))
    return running


def masked_scores(query_block, key_rows, allowed, score_scale):
    head_dim = query_block.shape[-1]
    scores = (
        jnp.einsum(
            "qhgd,hkd->qhgk",
            query_block,
            key_rows[..., :head_dim],
            preferred_element_type=jnp.float32,
        )
        * score_scale
    )
    return jnp.where(allowed, scores, NEG_FILL)


def with_ones(values):
    return jnp.concatenate([values, jnp.ones(values.shape[:-1] + (1,), values.dtype)], -1)


def dense_attention(
    query_block,
    cache_rows,
    span_rows,
    cache_pos,
    span_pos,
    prefix_limit,
    own_pos,
    valid_rows,
    sink_logit,
    score_scale,
):
    head_dim = query_block.shape[-1]
    cache_ok = (cache_pos < prefix_limit)[None, None, None, :]
    span_ok = (span_pos[None, :] <= own_pos[:, None])[:, None, None, :]
    cache_scores = masked_scores(query_block, cache_rows, cache_ok, score_scale)
    span_scores = masked_scores(query_block, span_rows, span_ok, score_scale)
    row_max = jnp.maximum(
        jnp.maximum(jnp.max(cache_scores, -1), jnp.max(span_scores, -1)), sink_logit[None]
    )
    cache_probs = jnp.exp(cache_scores - row_max[..., None]).astype(jnp.bfloat16)
    span_probs = jnp.exp(span_scores - row_max[..., None]).astype(jnp.bfloat16)
    acc = jnp.einsum(
        "qhgk,hkd->qhgd",
        cache_probs,
        with_ones(cache_rows[..., head_dim:]),
        preferred_element_type=jnp.float32,
    ) + jnp.einsum(
        "qhgk,hkd->qhgd",
        span_probs,
        with_ones(span_rows[..., head_dim:]),
        preferred_element_type=jnp.float32,
    )
    total = acc[..., head_dim] + jnp.exp(sink_logit[None] - row_max)
    acc = acc[..., :head_dim]
    result = acc / total[..., None]
    result = jnp.where(valid_rows[:, None, None, None], result, 0.0)
    return result.reshape(result.shape[0], -1).astype(jnp.bfloat16)


def empty_state(row_count, kv_heads, group_size, head_dim):
    return (
        jnp.full((row_count, kv_heads, group_size), NEG_FILL, jnp.float32),
        jnp.zeros((row_count, kv_heads, group_size), jnp.float32),
        jnp.zeros((row_count, kv_heads, group_size, head_dim), jnp.float32),
    )


def finish_rows(running_max, running_sum, running_acc, sink_logit, valid_rows):
    top_logit = jnp.maximum(running_max, sink_logit[None])
    shrink = jnp.exp(running_max - top_logit)
    denominator = running_sum * shrink + jnp.exp(sink_logit[None] - top_logit)
    result = running_acc * (shrink / denominator)[..., None]
    result = jnp.where(valid_rows[:, None, None, None], result, 0.0)
    return result.reshape(result.shape[0], -1).astype(jnp.bfloat16)


def column_norm(columns, norm_gain):
    widened = columns.astype(jnp.float32)
    return (
        widened
        * lax.rsqrt(jnp.mean(widened * widened, 0, keepdims=True) + 1e-05)
        * norm_gain[:, None]
    ).astype(jnp.bfloat16)


def expert_partials_t(normed_t, w_gate, w_up, w_down):
    gate_pre = jnp.einsum("dr,df->rf", normed_t, w_gate, preferred_element_type=jnp.float32)
    up_pre = jnp.einsum("dr,df->rf", normed_t, w_up, preferred_element_type=jnp.float32)
    active = swiglu_clamped(gate_pre, up_pre)
    return jnp.einsum("rf,fd->dr", active, w_down, preferred_element_type=jnp.float32).astype(
        jnp.bfloat16
    )


def pack_rows(table, rows, src_count, exp_local, capacity):
    packed = lax.dot_general(
        table, rows, (((0,), (0,)), ((), ())), preferred_element_type=jnp.float32
    ).astype(jnp.bfloat16)
    return packed.reshape(src_count, exp_local, capacity, -1)


def swiglu_clamped(gate_pre, up_pre):
    gated = jnp.minimum(gate_pre, 7.0)
    return ((jnp.clip(up_pre, -7.0, 7.0) + 1.0) * gated * jax.nn.sigmoid(1.702 * gated)).astype(
        jnp.bfloat16
    )


def weighted_mix(back_rows, slots, expert_weights):
    tok_rows, top_k = expert_weights.shape
    picked = back_rows[slots].reshape(tok_rows, top_k, -1)
    return jnp.einsum("tk,tkd->td", expert_weights, picked.astype(jnp.float32))


def per_device(
    queries,
    span_kv,
    cache_kv,
    prefix_len,
    span_len,
    sinks,
    out_proj,
    residual,
    norm_gain,
    expert_ids,
    expert_weights,
    w_gate,
    w_up,
    w_down,
    finished_pages,
    page_table,
):
    tok_rows = queries.shape[0]
    req_local, kv_heads, block_len, twice_dim = cache_kv.shape
    head_dim = twice_dim // 2
    group_size = queries.shape[1] // (kv_heads * head_dim)
    score_scale = head_dim ** (-0.5)
    blk_count = lax.axis_size("blk")
    req_count = lax.axis_size("req")
    src_count = req_count * blk_count
    span_rows = tok_rows * blk_count // req_local
    blk_index = lax.axis_index("blk")
    own_request = blk_index * tok_rows // span_rows
    own_pos = blk_index * tok_rows % span_rows + jnp.arange(tok_rows, dtype=jnp.int32)
    sink_logit = sinks.reshape(kv_heads, group_size)
    query_block = queries.reshape(tok_rows, kv_heads, group_size, head_dim)
    own_limit = lax.dynamic_index_in_dim(span_len, own_request, 0, keepdims=False)
    valid_rows = own_pos < own_limit
    prefix_limit = lax.dynamic_index_in_dim(prefix_len, own_request, 0, keepdims=False)
    own_cache = lax.dynamic_index_in_dim(cache_kv, own_request, 0, keepdims=False)
    payload = jnp.concatenate([own_cache, jnp.transpose(span_kv, (1, 0, 2))], 1)
    pieces = [payload]
    sources = [blk_index]
    for shift in range(1, blk_count):
        ring = [(i, (i + shift) % blk_count) for i in range(blk_count)]
        pieces.append(lax.ppermute(payload, "blk", ring))
        sources.append((blk_index - shift) % blk_count)
    cache_rows = jnp.concatenate([piece[:, :block_len] for piece in pieces], 1)
    span_keys = jnp.concatenate([piece[:, block_len:] for piece in pieces], 1)
    local_cache = jnp.arange(block_len, dtype=jnp.int32)
    local_span = jnp.arange(tok_rows, dtype=jnp.int32)
    cache_pos = jnp.concatenate([source * block_len + local_cache for source in sources])
    span_pos = jnp.concatenate([source * tok_rows + local_span for source in sources])
    attention = dense_attention(
        query_block,
        cache_rows,
        span_keys,
        cache_pos,
        span_pos,
        prefix_limit,
        own_pos,
        valid_rows,
        sink_logit,
        score_scale,
    )
    projected = jnp.dot(attention, out_proj, preferred_element_type=jnp.float32)
    exp_local = w_gate.shape[0]
    experts = exp_local * src_count
    top_k = expert_ids.shape[1]
    capacity = max(2, 2 * tok_rows * top_k // experts)
    flat_ids = expert_ids.reshape(-1)
    onehot = (flat_ids[:, None] == jnp.arange(experts, dtype=jnp.int32)[None, :]).astype(jnp.int32)
    ranks = jnp.sum((jnp.cumsum(onehot, 0) - onehot) * onehot, 1)
    slots = flat_ids * capacity + ranks
    table = jnp.any(
        slots.reshape(tok_rows, top_k)[:, :, None]
        == jnp.arange(experts * capacity, dtype=jnp.int32)[None, None, :],
        1,
    ).astype(jnp.bfloat16)
    head_index = lax.axis_index("head")
    column_count = residual.shape[1] // lax.axis_size("head")
    own_columns = lax.dynamic_slice_in_dim(residual, head_index * column_count, column_count, 1)
    head_count = lax.axis_size("head")
    pieces = jnp.transpose(
        projected.astype(jnp.bfloat16).reshape(tok_rows, head_count, column_count), (1, 0, 2)
    )
    pieces = lax.all_to_all(pieces, "head", split_axis=0, concat_axis=0, tiled=True)
    summed = jnp.sum(pieces.astype(jnp.float32), 0)
    hidden_cols = (own_columns.astype(jnp.float32) + summed).astype(jnp.bfloat16)
    outgoing = pack_rows(table, hidden_cols, src_count, exp_local, capacity)
    arrived = lax.all_to_all(outgoing, ("req", "blk"), split_axis=0, concat_axis=0, tiled=True)
    slot_total = experts * capacity
    arrived = jnp.transpose(arrived.reshape(slot_total, column_count))
    arrived = lax.all_gather(arrived, "head", axis=0, tiled=True)
    normed = column_norm(arrived, norm_gain)
    partial_out = expert_partials_t(normed, w_gate[0], w_up[0], w_down[0])
    partial_out = lax.psum_scatter(partial_out, "head", scatter_dimension=0, tiled=True)
    partial_out = jnp.transpose(partial_out).reshape(src_count, exp_local, capacity, column_count)
    returned = lax.all_to_all(partial_out, ("req", "blk"), split_axis=0, concat_axis=0, tiled=True)
    mixed = weighted_mix(returned.reshape(experts * capacity, -1), slots, expert_weights)
    layer_out = (hidden_cols.astype(jnp.float32) + mixed).astype(jnp.bfloat16)
    own_slot = lax.axis_index(("req", "blk"))
    pages_dev = finished_pages.shape[0]
    per_pair = pages_dev // src_count
    my_table = lax.dynamic_slice_in_dim(page_table, own_slot * pages_dev, pages_dev, 0)
    sort_key = my_table // pages_dev * pages_dev + jnp.arange(pages_dev, dtype=jnp.int32)
    ordering = jnp.argsort(sort_key)
    outbound = finished_pages[ordering]
    inbound = lax.all_to_all(
        outbound.reshape((src_count, per_pair) + outbound.shape[1:]),
        ("req", "blk"),
        split_axis=0,
        concat_axis=0,
        tiled=True,
    )
    inbound = inbound.reshape(finished_pages.shape)
    whole_table = page_table.reshape(src_count, pages_dev)
    marked = (
        jnp.where(whole_table // pages_dev == own_slot, 0, 1) * pages_dev
        + jnp.arange(pages_dev, dtype=jnp.int32)[None, :]
    )
    chosen = jnp.argsort(marked, axis=1)[:, :per_pair]
    arrived_slots = jnp.take_along_axis(whole_table, chosen, 1).reshape(-1) - own_slot * pages_dev
    moved_pages = inbound[jnp.argsort(arrived_slots)]
    return (layer_out, moved_pages)


def solution(mesh):
    in_specs = (
        P(("req", "blk"), "head"),
        P(("req", "blk"), "head", None),
        P("req", "head", "blk", None),
        P("req"),
        P("req"),
        P("head"),
        P("head", None),
        P(("req", "blk"), None),
        P(),
        P(("req", "blk"), None),
        P(("req", "blk"), None),
        P(("req", "blk"), None, "head"),
        P(("req", "blk"), None, "head"),
        P(("req", "blk"), "head", None),
        P(("req", "blk"), None, "head", None, None),
        P(),
    )
    out_specs = (P(("req", "blk"), "head"), P(("req", "blk"), None, "head", None, None))
    return jax.shard_map(
        per_device, mesh=mesh, in_specs=in_specs, out_specs=out_specs, check_vma=False
    )
```

```python
import math

import jax
import jax.numpy as jnp
from jax import lax
from jax.sharding import PartitionSpec as P

NEG_FILL = -1e30


def online_update(running, query_block, key_rows, allowed, score_scale):
    running_max, running_sum, running_acc = running
    head_dim = query_block.shape[-1]
    scores = (
        jnp.einsum(
            "qhgd,hkd->qhgk",
            query_block,
            key_rows[..., :head_dim],
            preferred_element_type=jnp.float32,
        )
        * score_scale
    )
    wide_mask = allowed[:, None, None, :]
    scores = jnp.where(wide_mask, scores, NEG_FILL)
    fresh_max = jnp.maximum(running_max, jnp.max(scores, -1))
    probs = jnp.where(wide_mask, jnp.exp(scores - fresh_max[..., None]), 0.0)
    factor = jnp.exp(running_max - fresh_max)
    running_sum = running_sum * factor + jnp.sum(probs, -1)
    running_acc = running_acc * factor[..., None] + jnp.einsum(
        "qhgk,hkd->qhgd",
        probs.astype(jnp.bfloat16),
        key_rows[..., head_dim:],
        preferred_element_type=jnp.float32,
    )
    return (fresh_max, running_sum, running_acc)


def sweep_cache(running, query_block, cache_rows, limit_pos, score_scale):
    kv_heads, row_count, twice_dim = cache_rows.shape
    block_len = math.gcd(512, row_count)
    block_count = row_count // block_len
    blocks = jnp.moveaxis(cache_rows.reshape(kv_heads, block_count, block_len, twice_dim), 1, 0)
    query_count = query_block.shape[0]

    def visit(state_now, scan_item):
        key_rows, block_index = scan_item
        key_pos = block_index * block_len + jnp.arange(block_len, dtype=jnp.int32)
        allowed = jnp.broadcast_to((key_pos < limit_pos)[None, :], (query_count, block_len))
        return (online_update(state_now, query_block, key_rows, allowed, score_scale), None)

    running, _ = lax.scan(visit, running, (blocks, jnp.arange(block_count, dtype=jnp.int32)))
    return running


def masked_scores(query_block, key_rows, allowed, score_scale):
    head_dim = query_block.shape[-1]
    scores = (
        jnp.einsum(
            "qhgd,hkd->qhgk",
            query_block,
            key_rows[..., :head_dim],
            preferred_element_type=jnp.float32,
        )
        * score_scale
    )
    return jnp.where(allowed, scores, NEG_FILL)


def with_ones(values):
    return jnp.concatenate([values, jnp.ones(values.shape[:-1] + (1,), values.dtype)], -1)


def dense_attention(
    query_block,
    cache_rows,
    span_rows,
    cache_pos,
    span_pos,
    prefix_limit,
    own_pos,
    valid_rows,
    sink_logit,
    score_scale,
):
    head_dim = query_block.shape[-1]
    cache_ok = (cache_pos < prefix_limit)[None, None, None, :]
    span_ok = (span_pos[None, :] <= own_pos[:, None])[:, None, None, :]
    cache_scores = masked_scores(query_block, cache_rows, cache_ok, score_scale)
    span_scores = masked_scores(query_block, span_rows, span_ok, score_scale)
    row_max = jnp.maximum(
        jnp.maximum(jnp.max(cache_scores, -1), jnp.max(span_scores, -1)), sink_logit[None]
    )
    cache_probs = jnp.exp(cache_scores - row_max[..., None]).astype(jnp.bfloat16)
    span_probs = jnp.exp(span_scores - row_max[..., None]).astype(jnp.bfloat16)
    acc = jnp.einsum(
        "qhgk,hkd->qhgd",
        cache_probs,
        with_ones(cache_rows[..., head_dim:]),
        preferred_element_type=jnp.float32,
    ) + jnp.einsum(
        "qhgk,hkd->qhgd",
        span_probs,
        with_ones(span_rows[..., head_dim:]),
        preferred_element_type=jnp.float32,
    )
    total = acc[..., head_dim] + jnp.exp(sink_logit[None] - row_max)
    acc = acc[..., :head_dim]
    result = acc / total[..., None]
    result = jnp.where(valid_rows[:, None, None, None], result, 0.0)
    return result.reshape(result.shape[0], -1).astype(jnp.bfloat16)


def blockwise_attention(query_block, pieces, masks, valid_rows, sink_logit, score_scale):
    head_dim = query_block.shape[-1]
    scores = [
        masked_scores(query_block, piece, mask[:, None, None, :], score_scale)
        for piece, mask in zip(pieces, masks)
    ]
    row_max = sink_logit[None]
    for block_scores in scores:
        row_max = jnp.maximum(row_max, jnp.max(block_scores, -1))
    acc = None
    for piece, block_scores in zip(pieces, scores):
        probs = jnp.exp(block_scores - row_max[..., None]).astype(jnp.bfloat16)
        part = jnp.einsum(
            "qhgk,hkd->qhgd",
            probs,
            with_ones(piece[..., head_dim:]),
            preferred_element_type=jnp.float32,
        )
        acc = part if acc is None else acc + part
    total = acc[..., head_dim] + jnp.exp(sink_logit[None] - row_max)
    result = acc[..., :head_dim] / total[..., None]
    result = jnp.where(valid_rows[:, None, None, None], result, 0.0)
    return result.reshape(result.shape[0], -1).astype(jnp.bfloat16)


def empty_state(row_count, kv_heads, group_size, head_dim):
    return (
        jnp.full((row_count, kv_heads, group_size), NEG_FILL, jnp.float32),
        jnp.zeros((row_count, kv_heads, group_size), jnp.float32),
        jnp.zeros((row_count, kv_heads, group_size, head_dim), jnp.float32),
    )


def finish_rows(running_max, running_sum, running_acc, sink_logit, valid_rows):
    top_logit = jnp.maximum(running_max, sink_logit[None])
    shrink = jnp.exp(running_max - top_logit)
    denominator = running_sum * shrink + jnp.exp(sink_logit[None] - top_logit)
    result = running_acc * (shrink / denominator)[..., None]
    result = jnp.where(valid_rows[:, None, None, None], result, 0.0)
    return result.reshape(result.shape[0], -1).astype(jnp.bfloat16)


def column_norm(columns, norm_gain):
    widened = columns.astype(jnp.float32)
    return (
        widened
        * lax.rsqrt(jnp.mean(widened * widened, 0, keepdims=True) + 1e-05)
        * norm_gain[:, None]
    ).astype(jnp.bfloat16)


def expert_partials_t(normed_t, w_gate, w_up, w_down):
    gate_pre = jnp.einsum("dr,df->rf", normed_t, w_gate, preferred_element_type=jnp.float32)
    up_pre = jnp.einsum("dr,df->rf", normed_t, w_up, preferred_element_type=jnp.float32)
    active = swiglu_clamped(gate_pre, up_pre)
    return jnp.einsum("rf,fd->dr", active, w_down, preferred_element_type=jnp.float32).astype(
        jnp.bfloat16
    )


def pack_rows(table, rows, src_count, exp_local, capacity):
    packed = lax.dot_general(
        table, rows, (((0,), (0,)), ((), ())), preferred_element_type=jnp.float32
    ).astype(jnp.bfloat16)
    return packed.reshape(src_count, exp_local, capacity, -1)


def swiglu_clamped(gate_pre, up_pre):
    gated = jnp.minimum(gate_pre, 7.0)
    return ((jnp.clip(up_pre, -7.0, 7.0) + 1.0) * gated * jax.nn.sigmoid(1.702 * gated)).astype(
        jnp.bfloat16
    )


def weighted_mix(back_rows, slots, expert_weights):
    tok_rows, top_k = expert_weights.shape
    picked = back_rows[slots].reshape(tok_rows, top_k, -1)
    return jnp.einsum("tk,tkd->td", expert_weights, picked.astype(jnp.float32))


def per_device(
    queries,
    span_kv,
    cache_kv,
    prefix_len,
    span_len,
    sinks,
    out_proj,
    residual,
    norm_gain,
    expert_ids,
    expert_weights,
    w_gate,
    w_up,
    w_down,
    finished_pages,
    page_table,
):
    tok_rows = queries.shape[0]
    req_local, kv_heads, block_len, twice_dim = cache_kv.shape
    head_dim = twice_dim // 2
    group_size = queries.shape[1] // (kv_heads * head_dim)
    score_scale = head_dim ** (-0.5)
    blk_count = lax.axis_size("blk")
    req_count = lax.axis_size("req")
    src_count = req_count * blk_count
    span_rows = tok_rows * blk_count // req_local
    blk_index = lax.axis_index("blk")
    own_request = blk_index * tok_rows // span_rows
    own_pos = blk_index * tok_rows % span_rows + jnp.arange(tok_rows, dtype=jnp.int32)
    sink_logit = sinks.reshape(kv_heads, group_size)
    query_block = queries.reshape(tok_rows, kv_heads, group_size, head_dim)
    own_limit = lax.dynamic_index_in_dim(span_len, own_request, 0, keepdims=False)
    valid_rows = own_pos < own_limit
    prefix_limit = lax.dynamic_index_in_dim(prefix_len, own_request, 0, keepdims=False)
    own_cache = lax.dynamic_index_in_dim(cache_kv, own_request, 0, keepdims=False)
    payload = jnp.concatenate([own_cache, jnp.transpose(span_kv, (1, 0, 2))], 1)
    pieces = [payload]
    sources = [blk_index]
    for shift in range(1, blk_count):
        ring = [(i, (i + shift) % blk_count) for i in range(blk_count)]
        pieces.append(lax.ppermute(payload, "blk", ring))
        sources.append((blk_index - shift) % blk_count)
    local_cache = jnp.arange(block_len, dtype=jnp.int32)
    local_span = jnp.arange(tok_rows, dtype=jnp.int32)
    masks = [
        jnp.concatenate(
            [
                jnp.broadcast_to(
                    (source * block_len + local_cache < prefix_limit)[None, :], (tok_rows, block_len)
                ),
                source * tok_rows + local_span[None, :] <= own_pos[:, None],
            ],
            1,
        )
        for source in sources
    ]
    attention = blockwise_attention(query_block, pieces, masks, valid_rows, sink_logit, score_scale)
    projected = jnp.dot(attention, out_proj, preferred_element_type=jnp.float32)
    exp_local = w_gate.shape[0]
    experts = exp_local * src_count
    top_k = expert_ids.shape[1]
    capacity = max(2, 2 * tok_rows * top_k // experts)
    flat_ids = expert_ids.reshape(-1)
    onehot = (flat_ids[:, None] == jnp.arange(experts, dtype=jnp.int32)[None, :]).astype(jnp.int32)
    ranks = jnp.sum((jnp.cumsum(onehot, 0) - onehot) * onehot, 1)
    slots = flat_ids * capacity + ranks
    table = jnp.any(
        slots.reshape(tok_rows, top_k)[:, :, None]
        == jnp.arange(experts * capacity, dtype=jnp.int32)[None, None, :],
        1,
    ).astype(jnp.bfloat16)
    head_index = lax.axis_index("head")
    column_count = residual.shape[1] // lax.axis_size("head")
    own_columns = lax.dynamic_slice_in_dim(residual, head_index * column_count, column_count, 1)
    head_count = lax.axis_size("head")
    pieces = jnp.transpose(
        projected.astype(jnp.bfloat16).reshape(tok_rows, head_count, column_count), (1, 0, 2)
    )
    pieces = lax.all_to_all(pieces, "head", split_axis=0, concat_axis=0, tiled=True)
    summed = jnp.sum(pieces.astype(jnp.float32), 0)
    hidden_cols = (own_columns.astype(jnp.float32) + summed).astype(jnp.bfloat16)
    outgoing = pack_rows(table, hidden_cols, src_count, exp_local, capacity)
    arrived = lax.all_to_all(outgoing, ("req", "blk"), split_axis=0, concat_axis=0, tiled=True)
    slot_total = experts * capacity
    arrived = jnp.transpose(arrived.reshape(slot_total, column_count))
    arrived = lax.all_gather(arrived, "head", axis=0, tiled=True)
    normed = column_norm(arrived, norm_gain)
    partial_out = expert_partials_t(normed, w_gate[0], w_up[0], w_down[0])
    partial_out = lax.psum_scatter(partial_out, "head", scatter_dimension=0, tiled=True)
    partial_out = jnp.transpose(partial_out).reshape(src_count, exp_local, capacity, column_count)
    returned = lax.all_to_all(partial_out, ("req", "blk"), split_axis=0, concat_axis=0, tiled=True)
    mixed = weighted_mix(returned.reshape(experts * capacity, -1), slots, expert_weights)
    layer_out = (hidden_cols.astype(jnp.float32) + mixed).astype(jnp.bfloat16)
    own_slot = lax.axis_index(("req", "blk"))
    pages_dev = finished_pages.shape[0]
    per_pair = pages_dev // src_count
    my_table = lax.dynamic_slice_in_dim(page_table, own_slot * pages_dev, pages_dev, 0)
    sort_key = my_table // pages_dev * pages_dev + jnp.arange(pages_dev, dtype=jnp.int32)
    ordering = jnp.argsort(sort_key)
    outbound = finished_pages[ordering]
    inbound = lax.all_to_all(
        outbound.reshape((src_count, per_pair) + outbound.shape[1:]),
        ("req", "blk"),
        split_axis=0,
        concat_axis=0,
        tiled=True,
    )
    inbound = inbound.reshape(finished_pages.shape)
    whole_table = page_table.reshape(src_count, pages_dev)
    marked = (
        jnp.where(whole_table // pages_dev == own_slot, 0, 1) * pages_dev
        + jnp.arange(pages_dev, dtype=jnp.int32)[None, :]
    )
    chosen = jnp.argsort(marked, axis=1)[:, :per_pair]
    arrived_slots = jnp.take_along_axis(whole_table, chosen, 1).reshape(-1) - own_slot * pages_dev
    moved_pages = inbound[jnp.argsort(arrived_slots)]
    return (layer_out, moved_pages)


def solution(mesh):
    in_specs = (
        P(("req", "blk"), "head"),
        P(("req", "blk"), "head", None),
        P("req", "head", "blk", None),
        P("req"),
        P("req"),
        P("head"),
        P("head", None),
        P(("req", "blk"), None),
        P(),
        P(("req", "blk"), None),
        P(("req", "blk"), None),
        P(("req", "blk"), None, "head"),
        P(("req", "blk"), None, "head"),
        P(("req", "blk"), "head", None),
        P(("req", "blk"), None, "head", None, None),
        P(),
    )
    out_specs = (P(("req", "blk"), "head"), P(("req", "blk"), None, "head", None, None))
    return jax.shard_map(
        per_device, mesh=mesh, in_specs=in_specs, out_specs=out_specs, check_vma=False
    )
```

```python
import math

import jax
import jax.numpy as jnp
from jax import lax
from jax.sharding import PartitionSpec as P

NEG_FILL = -1e30


def online_update(running, query_block, key_rows, allowed, score_scale):
    running_max, running_sum, running_acc = running
    head_dim = query_block.shape[-1]
    scores = (
        jnp.einsum(
            "qhgd,hkd->qhgk",
            query_block,
            key_rows[..., :head_dim],
            preferred_element_type=jnp.float32,
        )
        * score_scale
    )
    wide_mask = allowed[:, None, None, :]
    scores = jnp.where(wide_mask, scores, NEG_FILL)
    fresh_max = jnp.maximum(running_max, jnp.max(scores, -1))
    probs = jnp.where(wide_mask, jnp.exp(scores - fresh_max[..., None]), 0.0)
    factor = jnp.exp(running_max - fresh_max)
    running_sum = running_sum * factor + jnp.sum(probs, -1)
    running_acc = running_acc * factor[..., None] + jnp.einsum(
        "qhgk,hkd->qhgd",
        probs.astype(jnp.bfloat16),
        key_rows[..., head_dim:],
        preferred_element_type=jnp.float32,
    )
    return (fresh_max, running_sum, running_acc)


def sweep_cache(running, query_block, cache_rows, limit_pos, score_scale):
    kv_heads, row_count, twice_dim = cache_rows.shape
    block_len = math.gcd(512, row_count)
    block_count = row_count // block_len
    blocks = jnp.moveaxis(cache_rows.reshape(kv_heads, block_count, block_len, twice_dim), 1, 0)
    query_count = query_block.shape[0]

    def visit(state_now, scan_item):
        key_rows, block_index = scan_item
        key_pos = block_index * block_len + jnp.arange(block_len, dtype=jnp.int32)
        allowed = jnp.broadcast_to((key_pos < limit_pos)[None, :], (query_count, block_len))
        return (online_update(state_now, query_block, key_rows, allowed, score_scale), None)

    running, _ = lax.scan(visit, running, (blocks, jnp.arange(block_count, dtype=jnp.int32)))
    return running


def masked_scores(query_block, key_rows, allowed, score_scale):
    head_dim = query_block.shape[-1]
    scores = (
        jnp.einsum(
            "qhgd,hkd->qhgk",
            query_block,
            key_rows[..., :head_dim],
            preferred_element_type=jnp.float32,
        )
        * score_scale
    )
    return jnp.where(allowed, scores, NEG_FILL)


def with_ones(values):
    return jnp.concatenate([values, jnp.ones(values.shape[:-1] + (1,), values.dtype)], -1)


def dense_attention(
    query_block,
    cache_rows,
    span_rows,
    cache_pos,
    span_pos,
    prefix_limit,
    own_pos,
    valid_rows,
    sink_logit,
    score_scale,
):
    head_dim = query_block.shape[-1]
    cache_ok = (cache_pos < prefix_limit)[None, None, None, :]
    span_ok = (span_pos[None, :] <= own_pos[:, None])[:, None, None, :]
    cache_scores = masked_scores(query_block, cache_rows, cache_ok, score_scale)
    span_scores = masked_scores(query_block, span_rows, span_ok, score_scale)
    row_max = jnp.maximum(
        jnp.maximum(jnp.max(cache_scores, -1), jnp.max(span_scores, -1)), sink_logit[None]
    )
    cache_probs = jnp.exp(cache_scores - row_max[..., None]).astype(jnp.bfloat16)
    span_probs = jnp.exp(span_scores - row_max[..., None]).astype(jnp.bfloat16)
    acc = jnp.einsum(
        "qhgk,hkd->qhgd",
        cache_probs,
        with_ones(cache_rows[..., head_dim:]),
        preferred_element_type=jnp.float32,
    ) + jnp.einsum(
        "qhgk,hkd->qhgd",
        span_probs,
        with_ones(span_rows[..., head_dim:]),
        preferred_element_type=jnp.float32,
    )
    total = acc[..., head_dim] + jnp.exp(sink_logit[None] - row_max)
    acc = acc[..., :head_dim]
    result = acc / total[..., None]
    result = jnp.where(valid_rows[:, None, None, None], result, 0.0)
    return result.reshape(result.shape[0], -1).astype(jnp.bfloat16)


def blockwise_attention(query_block, pieces, masks, valid_rows, sink_logit, score_scale):
    head_dim = query_block.shape[-1]
    scores = [
        masked_scores(query_block, piece, mask[:, None, None, :], score_scale)
        for piece, mask in zip(pieces, masks)
    ]
    row_max = sink_logit[None]
    for block_scores in scores:
        row_max = jnp.maximum(row_max, jnp.max(block_scores, -1))
    acc = None
    for piece, block_scores in zip(pieces, scores):
        probs = jnp.exp(block_scores - row_max[..., None]).astype(jnp.bfloat16)
        part = jnp.einsum(
            "qhgk,hkd->qhgd",
            probs,
            with_ones(piece[..., head_dim:]),
            preferred_element_type=jnp.float32,
        )
        acc = part if acc is None else acc + part
    total = acc[..., head_dim] + jnp.exp(sink_logit[None] - row_max)
    result = acc[..., :head_dim] / total[..., None]
    result = jnp.where(valid_rows[:, None, None, None], result, 0.0)
    return result.reshape(result.shape[0], -1).astype(jnp.bfloat16)


def empty_state(row_count, kv_heads, group_size, head_dim):
    return (
        jnp.full((row_count, kv_heads, group_size), NEG_FILL, jnp.float32),
        jnp.zeros((row_count, kv_heads, group_size), jnp.float32),
        jnp.zeros((row_count, kv_heads, group_size, head_dim), jnp.float32),
    )


def finish_rows(running_max, running_sum, running_acc, sink_logit, valid_rows):
    top_logit = jnp.maximum(running_max, sink_logit[None])
    shrink = jnp.exp(running_max - top_logit)
    denominator = running_sum * shrink + jnp.exp(sink_logit[None] - top_logit)
    result = running_acc * (shrink / denominator)[..., None]
    result = jnp.where(valid_rows[:, None, None, None], result, 0.0)
    return result.reshape(result.shape[0], -1).astype(jnp.bfloat16)


def column_norm(columns, norm_gain):
    widened = columns.astype(jnp.float32)
    return (
        widened
        * lax.rsqrt(jnp.mean(widened * widened, 0, keepdims=True) + 1e-05)
        * norm_gain[:, None]
    ).astype(jnp.bfloat16)


def expert_partials_t(normed_t, w_gate, w_up, w_down):
    gate_pre = jnp.einsum("dr,df->rf", normed_t, w_gate, preferred_element_type=jnp.float32)
    up_pre = jnp.einsum("dr,df->rf", normed_t, w_up, preferred_element_type=jnp.float32)
    active = swiglu_clamped(gate_pre, up_pre)
    return jnp.einsum("rf,fd->dr", active, w_down, preferred_element_type=jnp.float32).astype(
        jnp.bfloat16
    )


def pack_rows(table, rows, src_count, exp_local, capacity):
    packed = lax.dot_general(
        table, rows, (((0,), (0,)), ((), ())), preferred_element_type=jnp.float32
    ).astype(jnp.bfloat16)
    return packed.reshape(src_count, exp_local, capacity, -1)


def swiglu_clamped(gate_pre, up_pre):
    gated = jnp.minimum(gate_pre, 7.0)
    return ((jnp.clip(up_pre, -7.0, 7.0) + 1.0) * gated * jax.nn.sigmoid(1.702 * gated)).astype(
        jnp.bfloat16
    )


def weighted_mix(back_rows, slots, expert_weights):
    tok_rows, top_k = expert_weights.shape
    picked = back_rows[slots].reshape(tok_rows, top_k, -1)
    return jnp.einsum("tk,tkd->td", expert_weights, picked.astype(jnp.float32))


def per_device(
    queries,
    span_kv,
    cache_kv,
    prefix_len,
    span_len,
    sinks,
    out_proj,
    residual,
    norm_gain,
    expert_ids,
    expert_weights,
    w_gate,
    w_up,
    w_down,
    finished_pages,
    page_table,
):
    tok_rows = queries.shape[0]
    req_local, kv_heads, block_len, twice_dim = cache_kv.shape
    head_dim = twice_dim // 2
    group_size = queries.shape[1] // (kv_heads * head_dim)
    score_scale = head_dim ** (-0.5)
    blk_count = lax.axis_size("blk")
    req_count = lax.axis_size("req")
    src_count = req_count * blk_count
    span_rows = tok_rows * blk_count // req_local
    blk_index = lax.axis_index("blk")
    own_request = blk_index * tok_rows // span_rows
    own_pos = blk_index * tok_rows % span_rows + jnp.arange(tok_rows, dtype=jnp.int32)
    sink_logit = sinks.reshape(kv_heads, group_size)
    query_block = queries.reshape(tok_rows, kv_heads, group_size, head_dim)
    own_limit = lax.dynamic_index_in_dim(span_len, own_request, 0, keepdims=False)
    valid_rows = own_pos < own_limit
    prefix_limit = lax.dynamic_index_in_dim(prefix_len, own_request, 0, keepdims=False)
    own_cache = lax.dynamic_index_in_dim(cache_kv, own_request, 0, keepdims=False)
    payload = jnp.concatenate([own_cache, jnp.transpose(span_kv, (1, 0, 2))], 1)
    pieces = [payload]
    sources = [blk_index]
    for shift in range(1, blk_count):
        ring = [(i, (i + shift) % blk_count) for i in range(blk_count)]
        pieces.append(lax.ppermute(payload, "blk", ring))
        sources.append((blk_index - shift) % blk_count)
    local_cache = jnp.arange(block_len, dtype=jnp.int32)
    local_span = jnp.arange(tok_rows, dtype=jnp.int32)
    is_cache = jnp.arange(block_len + tok_rows, dtype=jnp.int32) < block_len
    masks = []
    for source in sources:
        key_pos = jnp.concatenate([source * block_len + local_cache, source * tok_rows + local_span])
        masks.append(
            jnp.where(
                is_cache[None, :],
                (key_pos < prefix_limit)[None, :],
                key_pos[None, :] <= own_pos[:, None],
            )
        )
    attention = blockwise_attention(query_block, pieces, masks, valid_rows, sink_logit, score_scale)
    projected = jnp.dot(attention, out_proj, preferred_element_type=jnp.float32)
    exp_local = w_gate.shape[0]
    experts = exp_local * src_count
    top_k = expert_ids.shape[1]
    capacity = max(2, 2 * tok_rows * top_k // experts)
    flat_ids = expert_ids.reshape(-1)
    onehot = (flat_ids[:, None] == jnp.arange(experts, dtype=jnp.int32)[None, :]).astype(jnp.int32)
    ranks = jnp.sum((jnp.cumsum(onehot, 0) - onehot) * onehot, 1)
    slots = flat_ids * capacity + ranks
    table = jnp.any(
        slots.reshape(tok_rows, top_k)[:, :, None]
        == jnp.arange(experts * capacity, dtype=jnp.int32)[None, None, :],
        1,
    ).astype(jnp.bfloat16)
    head_index = lax.axis_index("head")
    column_count = residual.shape[1] // lax.axis_size("head")
    own_columns = lax.dynamic_slice_in_dim(residual, head_index * column_count, column_count, 1)
    head_count = lax.axis_size("head")
    pieces = jnp.transpose(
        projected.astype(jnp.bfloat16).reshape(tok_rows, head_count, column_count), (1, 0, 2)
    )
    pieces = lax.all_to_all(pieces, "head", split_axis=0, concat_axis=0, tiled=True)
    summed = jnp.sum(pieces.astype(jnp.float32), 0)
    hidden_cols = (own_columns.astype(jnp.float32) + summed).astype(jnp.bfloat16)
    outgoing = pack_rows(table, hidden_cols, src_count, exp_local, capacity)
    arrived = lax.all_to_all(outgoing, ("req", "blk"), split_axis=0, concat_axis=0, tiled=True)
    slot_total = experts * capacity
    arrived = jnp.transpose(arrived.reshape(slot_total, column_count))
    arrived = lax.all_gather(arrived, "head", axis=0, tiled=True)
    normed = column_norm(arrived, norm_gain)
    partial_out = expert_partials_t(normed, w_gate[0], w_up[0], w_down[0])
    partial_out = lax.psum_scatter(partial_out, "head", scatter_dimension=0, tiled=True)
    partial_out = jnp.transpose(partial_out).reshape(src_count, exp_local, capacity, column_count)
    returned = lax.all_to_all(partial_out, ("req", "blk"), split_axis=0, concat_axis=0, tiled=True)
    mixed = weighted_mix(returned.reshape(experts * capacity, -1), slots, expert_weights)
    layer_out = (hidden_cols.astype(jnp.float32) + mixed).astype(jnp.bfloat16)
    own_slot = lax.axis_index(("req", "blk"))
    pages_dev = finished_pages.shape[0]
    per_pair = pages_dev // src_count
    my_table = lax.dynamic_slice_in_dim(page_table, own_slot * pages_dev, pages_dev, 0)
    sort_key = my_table // pages_dev * pages_dev + jnp.arange(pages_dev, dtype=jnp.int32)
    ordering = jnp.argsort(sort_key)
    outbound = finished_pages[ordering]
    inbound = lax.all_to_all(
        outbound.reshape((src_count, per_pair) + outbound.shape[1:]),
        ("req", "blk"),
        split_axis=0,
        concat_axis=0,
        tiled=True,
    )
    inbound = inbound.reshape(finished_pages.shape)
    whole_table = page_table.reshape(src_count, pages_dev)
    marked = (
        jnp.where(whole_table // pages_dev == own_slot, 0, 1) * pages_dev
        + jnp.arange(pages_dev, dtype=jnp.int32)[None, :]
    )
    chosen = jnp.argsort(marked, axis=1)[:, :per_pair]
    arrived_slots = jnp.take_along_axis(whole_table, chosen, 1).reshape(-1) - own_slot * pages_dev
    moved_pages = inbound[jnp.argsort(arrived_slots)]
    return (layer_out, moved_pages)


def solution(mesh):
    in_specs = (
        P(("req", "blk"), "head"),
        P(("req", "blk"), "head", None),
        P("req", "head", "blk", None),
        P("req"),
        P("req"),
        P("head"),
        P("head", None),
        P(("req", "blk"), None),
        P(),
        P(("req", "blk"), None),
        P(("req", "blk"), None),
        P(("req", "blk"), None, "head"),
        P(("req", "blk"), None, "head"),
        P(("req", "blk"), "head", None),
        P(("req", "blk"), None, "head", None, None),
        P(),
    )
    out_specs = (P(("req", "blk"), "head"), P(("req", "blk"), None, "head", None, None))
    return jax.shard_map(
        per_device, mesh=mesh, in_specs=in_specs, out_specs=out_specs, check_vma=False
    )
```
